512 devices in a mesh: par: 32 (over z, core), perp: 16 (over x, y).
Axes of the slice: x: 4, y: 4, z: 16, core: 2. Of those that a mesh axis runs over, the one named last changes fastest.
Arguments:
- fields: float32 [2, 32, 8192, 256], P(None, 'par', 'perp'), may hold values from -6 to 6
- weight_bank: float32 [8, 128, 128], replicated, may hold values from -1 to 2, as said below
- dest_slab: int32 [2, 32, 128, 1], P(None, 'par', 'perp'), may hold values from 0 to 15; in each aligned block of 8 rows (0 to 7, 8 to 15, ..., all dimensions but the last counted through in order) at most 2 rows name the same one
- dest_tile: int32 [2, 32, 128], P(None, 'par', 'perp'), may hold values from 0 to 7
- tile_blocks: int32 [2, 32, 128, 2], P(None, 'par', 'perp'), may hold values from 0 to 7
- band_terms: float32 [2, 32], replicated, may hold values from 0.45 to 0.49
Outputs:
- gradient: float32 [2, 32, 8192, 256], P(None, 'par', 'perp')
The draws below stay inside these ranges and needn't reach their ends.
Inputs may be any that keep to these rules, and one draw needn't show every extreme that they name: `dest_slab`: in each direction and plane, at most 2 of the 8 tiles of one slab name the same destination slab, and in some slab exactly 2 do. `weight_bank`: each block is a dense real matrix.
All inputs are finite; a program needn't handle non-finite values.
Results may differ from the reference program's by a relative error of at most 0.0003.
Values sent between devices are 32-bit elements; how exact they have to be, the bound alone decides.
No kernel may reach another device: no remote copies, remote signals or barrier semaphores. Data moves between devices by JAX's collectives and lax.ppermute only.
A program may use at most 64 MiB of HBM per device.

```python
import math
import jax
import jax.numpy as jnp
import numpy as np
from jax import lax

TILE = 128
NB = 8
NY = 256
PLANES = 32
NX = 8192
TPS = 8
TILES = 128
CAP = 2
N_PERP = 16


def draw_weight_bank(key, part):
    identity = jnp.eye(TILE, dtype=jnp.float32)
    spread = 0.5 / math.sqrt(TILE)
    noise = jax.random.normal(key, (NB, TILE, TILE), jnp.float32)
    return identity[None] + spread * noise


def place_ends(values, key, low, high):
    place = [jax.random.randint(jax.random.fold_in(key, axis), (), 0, length) for axis, length in enumerate(values.shape)]
    main_axis = values.shape.index(max(values.shape))
    neighbour = place[:main_axis] + [(place[main_axis] + 1) % values.shape[main_axis]] + place[main_axis + 1:]
    return values.at[tuple(place)].set(low).at[tuple(neighbour)].set(high)


def steps_of(stream_key, extent, split, smallest, top_value):
    def one(axis_at, shards_of):
        heights = jax.random.uniform(jax.random.fold_in(jax.random.fold_in(stream_key, 6), axis_at), (shards_of,), jnp.float32, smallest / len(split), top_value / len(split))
        return jnp.repeat(jnp.exp(heights), extent[axis_at] // shards_of).reshape((-1,) + (1,) * (len(extent) - axis_at - 1))

    level = one(*split[0])
    for cut in split[1:]:
        level = level * one(*cut)
    return level


def shared_out(key, own, number, rows, number_of, top, most, lean):
    sequence = jax.random.permutation(key, number_of)
    crowded, usual = portions_of(number_of, rows * top, most, lean, True), portions_of(number_of, rows * top, most, lean, False)
    places = jnp.arange(number_of)

    def named(tallies, rotation):
        used = int((tallies > 0).sum())
        fixed = max(1, used // 4)
        passed = fixed + (places - fixed + rotation * (used - fixed)) % max(1, number_of - fixed)
        return jnp.zeros((number_of,), jnp.int32).at[sequence[jnp.where(places < fixed, places, passed)]].set(jnp.asarray(tallies, jnp.int32))

    tallies = jnp.where(number % 4 == 0, named(crowded, number // 4), named(usual, number - number // 4 - 1))
    mixed = jax.random.permutation(jax.random.fold_in(own, 3), number_of)
    giver, sink = mixed[0:number_of // 2 * 2:2], mixed[1:number_of // 2 * 2:2]
    margin = jnp.minimum(tallies[giver] - 1, most - tallies[sink]) // 2
    margin = jnp.where((giver == sequence[0]) | (sink == sequence[0]) | (tallies[sink] == 0), 0, jnp.maximum(margin, 0))
    passed = jax.random.randint(jax.random.fold_in(own, 4), (number_of // 2,), 0, 1 << 20) % (margin + 1)
    tallies = tallies.at[giver].add(-passed).at[sink].add(passed)
    items = jnp.searchsorted(jnp.cumsum(tallies), jnp.arange(rows * top), side="right").astype(jnp.int32)
    grid = items.reshape(top, rows).T
    grid = grid[jax.random.permutation(jax.random.fold_in(own, 1), rows)]
    rotation = jax.random.randint(jax.random.fold_in(own, 2), (rows, 1), 0, top)
    return jnp.take_along_axis(grid, (jnp.arange(top)[None, :] + rotation) % top, axis=1)


def portions_of(count, total, limit, lean, full):
    loads = [(1 << 20) // math.isqrt(grade ** lean) + 1 for grade in range(1, count + 1)]
    largest = limit if full else min(limit, max(-(-total // count), total * loads[0] // sum(loads)))
    least = 1 if total - largest >= count - 1 else 0
    given, surplus = [largest] + [least] * (count - 1), total - largest - least * (count - 1)
    while surplus > 0:
        movable = [i for i in range(1, count) if given[i] < largest] or [i for i in range(1, count) if given[i] < limit]
        pool, remaining = sum([loads[i] for i in movable]), surplus
        for i in movable:
            addition = min(limit - given[i], max(1, remaining * loads[i] // pool), surplus)
            given[i] = given[i] + addition
            surplus = surplus - addition
    return np.array(given)


def scatter_about(stream_key, shape, scale, most, pieces=(), kind=jnp.bfloat16):
    values = scale * jax.random.normal(stream_key, shape, jnp.float32)
    if pieces:
        values = values * steps_of(stream_key, shape, pieces, -0.22, 0.18)
    return jnp.clip(values, -most, most).astype(kind)


def setup_inputs(seed: int = 0) -> dict:
    splits = jax.random.split(jax.random.key(seed), 7)
    fields = scatter_about(splits[0], (2, PLANES, NX, NY), 1.0, 6.0, ((1, 32), (2, 16)), jnp.float32)
    weight_bank = draw_weight_bank(jax.random.fold_in(splits[6], 71), 0)
    dest_slab_keys = jax.random.split(jax.random.fold_in(splits[2], 1), 2 * PLANES * TILES // TPS)
    dest_slab_turns = jax.random.permutation(jax.random.fold_in(splits[2], 3), 2 * PLANES * TILES // TPS)
    dest_slab = jax.vmap(lambda own, number: shared_out(jax.random.fold_in(splits[2], 2), own, number, TPS, N_PERP, 1, CAP, 2))(dest_slab_keys, dest_slab_turns).reshape((2, PLANES, TILES, 1))
    dest_tile = place_ends(jax.random.randint(splits[3], (2, PLANES, TILES), 0, TPS), jax.random.fold_in(splits[3], 1), 0, TPS - 1).astype(jnp.int32)
    tile_blocks = place_ends(jax.random.randint(splits[4], (2, PLANES, TILES, 2), 0, NB), jax.random.fold_in(splits[4], 1), 0, NB - 1).astype(jnp.int32)
    band_terms = jnp.clip(jax.random.uniform(splits[5], (2, PLANES), jnp.float32, 0.45, 0.49), 0.45, 0.49)
    return {"fields": fields, "weight_bank": weight_bank, "dest_slab": dest_slab, "dest_tile": dest_tile, "tile_blocks": tile_blocks, "band_terms": band_terms}


PRECISE = lax.Precision.HIGHEST
KAPPA = 0.125


def to_tiles(plane_data):
    shaped = plane_data.reshape(NX // TILE, TILE, NY // TILE, TILE)
    return shaped.transpose(0, 2, 1, 3).reshape(TILES, TILE, TILE)


def from_tiles(tile_set):
    shaped = tile_set.reshape(NX // TILE, NY // TILE, TILE, TILE)
    return shaped.transpose(0, 2, 1, 3).reshape(NX, NY)


def smooth(plane_data):
    padded = jnp.pad(plane_data, 1)
    beside_all = padded[2:, 1:-1] + padded[:-2, 1:-1] + padded[1:-1, 2:] + padded[1:-1, :-2]
    return plane_data + KAPPA * (beside_all - 4.0 * plane_data)


def coefficients(band_terms):
    plane_total = band_terms.shape[1]
    position = jnp.arange(plane_total, dtype=jnp.int32)
    lower_band = jnp.where(position > 0, band_terms[0], 0.0)
    upper_band = jnp.where(position < plane_total - 1, band_terms[1], 0.0)

    def advance(previous, element):
        lower_now, upper_now = element
        pivot_now = 1.0 - lower_now * previous
        ratio_now = upper_now / pivot_now
        return ratio_now, (pivot_now, ratio_now)

    _, (pivots, ratios) = lax.scan(advance, jnp.zeros((), jnp.float32), (lower_band, upper_band))
    return lower_band, pivots, ratios


def reference(fields, weight_bank, dest_slab, dest_tile, tile_blocks, band_terms):
    def deposit_plane(element):
        plane_data, slab_row, tile_row, block_row = element
        tile_set = to_tiles(plane_data)
        shifted = jnp.einsum('sij,sjk->sik', weight_bank[block_row[:, 0]], tile_set, precision=PRECISE)
        shifted = jnp.einsum('sik,slk->sil', shifted, weight_bank[block_row[:, 1]], precision=PRECISE)
        target = slab_row * TPS + tile_row
        onehot = (jnp.arange(TILES, dtype=jnp.int32)[:, None] == target[None, :]).astype(jnp.float32)
        return from_tiles(jnp.einsum('ts,sij->tij', onehot, shifted, precision=PRECISE))

    upward = lax.map(deposit_plane, (fields[0], dest_slab[0, :, :, 0], dest_tile[0], tile_blocks[0]))
    downward = lax.map(deposit_plane, (fields[1], dest_slab[1, :, :, 0], dest_tile[1], tile_blocks[1]))
    blank_plane = jnp.zeros((1, NX, NY), jnp.float32)
    mapped_up = jnp.concatenate((blank_plane, upward[:-1]), axis=0)
    mapped_down = jnp.concatenate((downward[1:], blank_plane), axis=0)
    smooth_up = jax.vmap(smooth)(mapped_up)
    smooth_down = jax.vmap(smooth)(mapped_down)
    right_side = jnp.stack((fields[0] - smooth_up, -(fields[1] - smooth_down)))
    lower_band, pivots, ratios = coefficients(band_terms)
    stacked = jnp.moveaxis(right_side, 1, 0)

    def forward(previous, element):
        current_value, lower_now, pivot_now = element
        current = (current_value - lower_now * previous) / pivot_now
        return current, current

    zeros_pair = jnp.zeros((2, NX, NY), jnp.float32)
    _, eliminated = lax.scan(forward, zeros_pair, (stacked, lower_band, pivots))

    def backward(following, element):
        current_value, ratio_now = element
        current = current_value - ratio_now * following
        return current, current

    _, solved = lax.scan(backward, zeros_pair, (eliminated, ratios), reverse=True)
    return jnp.moveaxis(solved, 0, 1)
```

```python
import jax
import jax.numpy as jnp
from jax import lax
from jax.sharding import PartitionSpec as P

TILE = 128


PRECISE = lax.Precision.HIGHEST
KAPPA = 0.125


def extended(block, sides, width):
    for axis, dim in sides:
        count = lax.axis_size(axis)
        forward = [(i, i + 1) for i in range(count - 1)]
        backward = [(target, source) for source, target in forward]
        low = lax.ppermute(
            lax.slice_in_dim(block, block.shape[dim] - width, None, axis=dim), axis, forward
        )
        high = lax.ppermute(lax.slice_in_dim(block, 0, width, axis=dim), axis, backward)
        block = jnp.concatenate([low, block, high], axis=dim)
    return block


def split_tiles(plane_pair):
    field_count, row_count, col_count = plane_pair.shape
    shaped = plane_pair.reshape(field_count, row_count // TILE, TILE, col_count // TILE, TILE)
    return shaped.transpose(0, 1, 3, 2, 4).reshape(field_count, -1, TILE, TILE)


def join_tiles(tile_set, row_count, col_count):
    field_count = tile_set.shape[0]
    shaped = tile_set.reshape(field_count, row_count // TILE, col_count // TILE, TILE, TILE)
    return shaped.transpose(0, 1, 3, 2, 4).reshape(field_count, row_count, col_count)


def coefficients(band_terms):
    plane_total = band_terms.shape[1]
    lower, pivots, ratios = [], [], []
    previous = jnp.zeros((), jnp.float32)
    for p in range(plane_total):
        lower_now = band_terms[0, p] if p > 0 else jnp.zeros((), jnp.float32)
        upper_now = band_terms[1, p] if p < plane_total - 1 else jnp.zeros((), jnp.float32)
        pivot_now = 1.0 - lower_now * previous
        ratio_now = upper_now / pivot_now
        lower.append(lower_now)
        pivots.append(pivot_now)
        ratios.append(ratio_now)
        previous = ratio_now
    return lower, pivots, ratios


def slot_labels(dest_slabs, target, peer_count, capacity):
    tile_count = dest_slabs.shape[-1]
    position = jnp.arange(tile_count, dtype=jnp.int32)
    earlier = position[:, None] > position[None, :]
    shared = dest_slabs[..., :, None] == dest_slabs[..., None, :]
    slot_rank = jnp.sum((shared & earlier).astype(jnp.int32), axis=-1)
    peer_ids = jnp.arange(peer_count, dtype=jnp.int32)
    slot_ids = jnp.arange(capacity, dtype=jnp.int32)
    chosen = (dest_slabs[..., None, None, :] == peer_ids[:, None, None]) & (
        slot_rank[..., None, None, :] == slot_ids[None, :, None]
    )
    return chosen


def local(fields, weight_bank, dest_slab, dest_tile, tile_blocks, band_terms):
    peer_count = lax.axis_size("perp")
    plane_count = lax.axis_size("par")
    row_count = fields.shape[2]
    col_count = fields.shape[3]
    local_pair = fields[:, 0]
    tile_set = split_tiles(local_pair)
    tile_count = tile_set.shape[1]
    capacity = max(2, (tile_count + peer_count - 1) // peer_count)
    dest_slabs = dest_slab[:, 0, :, 0]
    target = dest_tile[:, 0, :]
    left_index = tile_blocks[:, 0, :, 0]
    right_index = tile_blocks[:, 0, :, 1]

    left_block = jnp.take(weight_bank, left_index, axis=0, mode="clip")
    right_block = jnp.take(weight_bank, right_index, axis=0, mode="clip")
    shifted = jnp.einsum("dsij,dsjk->dsik", left_block, tile_set, precision=PRECISE)
    moved = jnp.einsum("dsik,dslk->dsil", shifted, right_block, precision=PRECISE)

    chosen = slot_labels(dest_slabs, target, peer_count, capacity)
    picker = chosen.astype(jnp.float32)
    packed = jnp.einsum("dpcs,dsij->dpcij", picker, moved, precision=PRECISE)
    moved_tiles = lax.all_to_all(packed, "perp", split_axis=1, concat_axis=1, tiled=True)

    all_slabs = lax.all_gather(dest_slabs, "perp", axis=1, tiled=True)
    all_targets = lax.all_gather(target, "perp", axis=1, tiled=True)
    field_count = all_slabs.shape[0]
    all_slabs = all_slabs.reshape(field_count, peer_count, tile_count)
    all_targets = all_targets.reshape(field_count, peer_count, tile_count)
    source_chosen = slot_labels(all_slabs, all_targets, peer_count, capacity)
    me = lax.axis_index("perp")
    mine = source_chosen[:, :, me]
    arrived_target = (
        jnp.sum(mine.astype(jnp.int32) * (all_targets[:, :, None, :] + 1), axis=-1) - 1
    )
    position = jnp.arange(tile_count, dtype=jnp.int32)
    flattened = moved_tiles.reshape(field_count, peer_count * capacity, TILE, TILE)
    flat_target = arrived_target.reshape(field_count, peer_count * capacity)
    landing = (flat_target[:, None, :] == position[None, :, None]).astype(jnp.float32)
    summed = jnp.einsum("dts,dsij->dtij", landing, flattened, precision=PRECISE)
    deposit = join_tiles(summed, row_count, col_count)

    upward = [(i, i + 1) for i in range(plane_count - 1)]
    downward = [(i + 1, i) for i in range(plane_count - 1)]
    mapped = jnp.stack(
        (lax.ppermute(deposit[0], "par", upward), lax.ppermute(deposit[1], "par", downward))
    )
    rimmed = extended(mapped, (("perp", 1),), 1)
    padded = jnp.pad(rimmed, ((0, 0), (0, 0), (1, 1)))
    beside_all = (
        padded[:, 2:, 1:-1] + padded[:, :-2, 1:-1] + padded[:, 1:-1, 2:] + padded[:, 1:-1, :-2]
    )
    smoothed = mapped + KAPPA * (beside_all - 4.0 * mapped)
    orient = jnp.array([1.0, -1.0], jnp.float32)[:, None, None]
    right_side = orient * (local_pair - smoothed)
    lower, pivots, ratios = coefficients(band_terms)
    column_block = lax.all_to_all(
        right_side[:, None], "par", split_axis=2, concat_axis=1, tiled=True
    )
    depth_count = column_block.shape[1]
    eliminated = []
    previous = None
    for p in range(depth_count):
        current = column_block[:, p]
        if previous is not None:
            current = current - lower[p] * previous
        current = current / pivots[p]
        eliminated.append(current)
        previous = current
    solved = [None] * depth_count
    following = None
    for p in reversed(range(depth_count)):
        current = eliminated[p]
        if following is not None:
            current = current - ratios[p] * following
        solved[p] = current
        following = current
    solved = jnp.stack(solved, axis=1)
    result = lax.all_to_all(solved, "par", split_axis=1, concat_axis=2, tiled=True)
    return result


def solution(mesh):
    placed = (
        P(None, "par", "perp", None),
        P(),
        P(None, "par", "perp", None),
        P(None, "par", "perp"),
        P(None, "par", "perp", None),
        P(),
    )
    return jax.shard_map(
        local, mesh=mesh, in_specs=placed, out_specs=P(None, "par", "perp", None), check_vma=False
    )
```

```python
import jax
import jax.numpy as jnp
from jax import lax
from jax.experimental import pallas as pl
from jax.experimental.pallas import tpu as pltpu
from jax.sharding import PartitionSpec as P

TILE = 128


PRECISE = lax.Precision.HIGHEST
KAPPA = 0.125


def extended(block, sides, width):
    for axis, dim in sides:
        count = lax.axis_size(axis)
        forward = [(i, i + 1) for i in range(count - 1)]
        backward = [(target, source) for source, target in forward]
        low = lax.ppermute(
            lax.slice_in_dim(block, block.shape[dim] - width, None, axis=dim), axis, forward
        )
        high = lax.ppermute(lax.slice_in_dim(block, 0, width, axis=dim), axis, backward)
        block = jnp.concatenate([low, block, high], axis=dim)
    return block


def split_tiles(plane_pair):
    field_count, row_count, col_count = plane_pair.shape
    shaped = plane_pair.reshape(field_count, row_count // TILE, TILE, col_count // TILE, TILE)
    return shaped.transpose(0, 1, 3, 2, 4).reshape(field_count, -1, TILE, TILE)


def join_tiles(tile_set, row_count, col_count):
    field_count = tile_set.shape[0]
    shaped = tile_set.reshape(field_count, row_count // TILE, col_count // TILE, TILE, TILE)
    return shaped.transpose(0, 1, 3, 2, 4).reshape(field_count, row_count, col_count)


def coefficients(band_terms):
    plane_total = band_terms.shape[1]
    lower, pivots, ratios = [], [], []
    previous = jnp.zeros((), jnp.float32)
    for p in range(plane_total):
        lower_now = band_terms[0, p] if p > 0 else jnp.zeros((), jnp.float32)
        upper_now = band_terms[1, p] if p < plane_total - 1 else jnp.zeros((), jnp.float32)
        pivot_now = 1.0 - lower_now * previous
        ratio_now = upper_now / pivot_now
        lower.append(lower_now)
        pivots.append(pivot_now)
        ratios.append(ratio_now)
        previous = ratio_now
    return lower, pivots, ratios


def slot_labels(dest_slabs, target, peer_count, capacity):
    tile_count = dest_slabs.shape[-1]
    position = jnp.arange(tile_count, dtype=jnp.int32)
    earlier = position[:, None] > position[None, :]
    shared = dest_slabs[..., :, None] == dest_slabs[..., None, :]
    slot_rank = jnp.sum((shared & earlier).astype(jnp.int32), axis=-1)
    peer_ids = jnp.arange(peer_count, dtype=jnp.int32)
    slot_ids = jnp.arange(capacity, dtype=jnp.int32)
    chosen = (dest_slabs[..., None, None, :] == peer_ids[:, None, None]) & (
        slot_rank[..., None, None, :] == slot_ids[None, :, None]
    )
    return chosen


def thomas_kernel(lower_ref, pivot_ref, ratio_ref, rhs_ref, out_ref):
    depth = rhs_ref.shape[1]
    previous = rhs_ref[:, 0] / pivot_ref[0]
    out_ref[:, 0] = previous
    for p in range(1, depth):
        previous = (rhs_ref[:, p] - lower_ref[p] * previous) / pivot_ref[p]
        out_ref[:, p] = previous
    following = previous
    for p in reversed(range(depth - 1)):
        following = out_ref[:, p] - ratio_ref[p] * following
        out_ref[:, p] = following


def thomas(rhs, lower, pivots, ratios):
    scalar = pl.BlockSpec(memory_space=pltpu.SMEM)
    whole = pl.BlockSpec(memory_space=pltpu.VMEM)
    return pl.pallas_call(
        thomas_kernel,
        out_shape=jax.ShapeDtypeStruct(rhs.shape, rhs.dtype),
        in_specs=[scalar, scalar, scalar, whole],
        out_specs=whole,
    )(lower, pivots, ratios, rhs)


def local(fields, weight_bank, dest_slab, dest_tile, tile_blocks, band_terms):
    peer_count = lax.axis_size("perp")
    plane_count = lax.axis_size("par")
    row_count = fields.shape[2]
    col_count = fields.shape[3]
    local_pair = fields[:, 0]
    tile_set = split_tiles(local_pair)
    tile_count = tile_set.shape[1]
    capacity = max(2, (tile_count + peer_count - 1) // peer_count)
    dest_slabs = dest_slab[:, 0, :, 0]
    target = dest_tile[:, 0, :]
    left_index = tile_blocks[:, 0, :, 0]
    right_index = tile_blocks[:, 0, :, 1]

    left_block = jnp.take(weight_bank, left_index, axis=0, mode="clip")
    right_block = jnp.take(weight_bank, right_index, axis=0, mode="clip")
    shifted = jnp.einsum("dsij,dsjk->dsik", left_block, tile_set, precision=PRECISE)
    moved = jnp.einsum("dsik,dslk->dsil", shifted, right_block, precision=PRECISE)

    chosen = slot_labels(dest_slabs, target, peer_count, capacity)
    picker = chosen.astype(jnp.float32)
    packed = jnp.einsum("dpcs,dsij->dpcij", picker, moved, precision=PRECISE)
    moved_tiles = lax.all_to_all(packed, "perp", split_axis=1, concat_axis=1, tiled=True)

    slot_target = jnp.sum(chosen.astype(jnp.int32) * (target[:, None, None, :] + 1), axis=3) - 1
    arrived_target = lax.all_to_all(slot_target, "perp", split_axis=1, concat_axis=1, tiled=True)
    field_count = tile_set.shape[0]
    position = jnp.arange(tile_count, dtype=jnp.int32)
    flattened = moved_tiles.reshape(field_count, peer_count * capacity, TILE, TILE)
    flat_target = arrived_target.reshape(field_count, peer_count * capacity)
    landing = (flat_target[:, None, :] == position[None, :, None]).astype(jnp.float32)
    summed = jnp.einsum("dts,dsij->dtij", landing, flattened, precision=PRECISE)
    deposit = join_tiles(summed, row_count, col_count)

    upward = [(i, i + 1) for i in range(plane_count - 1)]
    downward = [(i + 1, i) for i in range(plane_count - 1)]
    mapped = jnp.stack(
        (lax.ppermute(deposit[0], "par", upward), lax.ppermute(deposit[1], "par", downward))
    )
    rimmed = extended(mapped, (("perp", 1),), 1)
    padded = jnp.pad(rimmed, ((0, 0), (0, 0), (1, 1)))
    beside_all = (
        padded[:, 2:, 1:-1] + padded[:, :-2, 1:-1] + padded[:, 1:-1, 2:] + padded[:, 1:-1, :-2]
    )
    smoothed = mapped + KAPPA * (beside_all - 4.0 * mapped)
    orient = jnp.array([1.0, -1.0], jnp.float32)[:, None, None]
    right_side = orient * (local_pair - smoothed)
    lower, pivots, ratios = coefficients(band_terms)
    column_block = lax.all_to_all(
        right_side[:, None], "par", split_axis=2, concat_axis=1, tiled=True
    )
    solved = thomas(column_block, jnp.stack(lower), jnp.stack(pivots), jnp.stack(ratios))
    result = lax.all_to_all(solved, "par", split_axis=1, concat_axis=2, tiled=True)
    return result


def solution(mesh):
    placed = (
        P(None, "par", "perp", None),
        P(),
        P(None, "par", "perp", None),
        P(None, "par", "perp"),
        P(None, "par", "perp", None),
        P(),
    )
    return jax.shard_map(
        local, mesh=mesh, in_specs=placed, out_specs=P(None, "par", "perp", None), check_vma=False
    )
```

```python
import jax
import jax.numpy as jnp
from jax import lax
from jax.experimental import pallas as pl
from jax.experimental.pallas import tpu as pltpu
from jax.sharding import PartitionSpec as P

TILE = 128


PRECISE = lax.Precision.HIGHEST
KAPPA = 0.125


def split_tiles(plane_pair):
    field_count, row_count, col_count = plane_pair.shape
    shaped = plane_pair.reshape(field_count, row_count // TILE, TILE, col_count // TILE, TILE)
    return shaped.transpose(0, 1, 3, 2, 4).reshape(field_count, -1, TILE, TILE)


def join_tiles(tile_set, row_count, col_count):
    field_count = tile_set.shape[0]
    shaped = tile_set.reshape(field_count, row_count // TILE, col_count // TILE, TILE, TILE)
    return shaped.transpose(0, 1, 3, 2, 4).reshape(field_count, row_count, col_count)


def coefficients(band_terms):
    plane_total = band_terms.shape[1]
    lower, pivots, ratios = [], [], []
    previous = jnp.zeros((), jnp.float32)
    for p in range(plane_total):
        lower_now = band_terms[0, p] if p > 0 else jnp.zeros((), jnp.float32)
        upper_now = band_terms[1, p] if p < plane_total - 1 else jnp.zeros((), jnp.float32)
        pivot_now = 1.0 - lower_now * previous
        ratio_now = upper_now / pivot_now
        lower.append(lower_now)
        pivots.append(pivot_now)
        ratios.append(ratio_now)
        previous = ratio_now
    return lower, pivots, ratios


def slot_labels(dest_slabs, peer_count, capacity):
    tile_count = dest_slabs.shape[-1]
    position = jnp.arange(tile_count, dtype=jnp.int32)
    earlier = position[:, None] > position[None, :]
    shared = dest_slabs[..., :, None] == dest_slabs[..., None, :]
    slot_rank = jnp.sum((shared & earlier).astype(jnp.int32), axis=-1)
    peer_ids = jnp.arange(peer_count, dtype=jnp.int32)
    slot_ids = jnp.arange(capacity, dtype=jnp.int32)
    chosen = (dest_slabs[..., None, None, :] == peer_ids[:, None, None]) & (
        slot_rank[..., None, None, :] == slot_ids[None, :, None]
    )
    return chosen


def thomas_kernel(lower_ref, pivot_ref, ratio_ref, rhs_ref, out_ref):
    depth = rhs_ref.shape[0]
    previous = rhs_ref[0] / pivot_ref[0]
    out_ref[0] = previous
    for p in range(1, depth):
        previous = (rhs_ref[p] - lower_ref[p] * previous) / pivot_ref[p]
        out_ref[p] = previous
    following = previous
    for p in reversed(range(depth - 1)):
        following = out_ref[p] - ratio_ref[p] * following
        out_ref[p] = following


def thomas(rhs, lower, pivots, ratios):
    scalar = pl.BlockSpec(memory_space=pltpu.SMEM)
    whole = pl.BlockSpec(memory_space=pltpu.VMEM)
    return pl.pallas_call(
        thomas_kernel,
        out_shape=jax.ShapeDtypeStruct(rhs.shape, rhs.dtype),
        in_specs=[scalar, scalar, scalar, whole],
        out_specs=whole,
    )(lower, pivots, ratios, rhs)


def smooth_slab(plane, above_row, below_row):
    row_count, col_count = plane.shape
    zero_col = jnp.zeros((row_count, 1), plane.dtype)
    above = jnp.concatenate([above_row, plane[:-1]], axis=0)
    below = jnp.concatenate([plane[1:], below_row], axis=0)
    left = jnp.concatenate([zero_col, plane[:, :-1]], axis=1)
    right = jnp.concatenate([plane[:, 1:], zero_col], axis=1)
    beside_all = below + above + right + left
    return plane + KAPPA * (beside_all - 4.0 * plane)


def local(fields, weight_bank, dest_slab, dest_tile, tile_blocks, band_terms):
    peer_count = lax.axis_size("perp")
    plane_count = lax.axis_size("par")
    field_count, _, row_count, col_count = fields.shape
    local_pair = fields[:, 0]
    tile_set = split_tiles(local_pair)
    tile_count = tile_set.shape[1]
    capacity = max(2, (tile_count + peer_count - 1) // peer_count)
    dest_slabs = dest_slab[:, 0, :, 0]
    target = dest_tile[:, 0, :]
    left_index = tile_blocks[:, 0, :, 0]
    right_index = tile_blocks[:, 0, :, 1]

    left_block = jnp.take(weight_bank, left_index, axis=0, mode="clip")
    right_block = jnp.take(weight_bank, right_index, axis=0, mode="clip")
    shifted = jnp.einsum("dsij,dsjk->dsik", left_block, tile_set, precision=PRECISE)
    moved = jnp.einsum("dsik,dslk->dsil", shifted, right_block, precision=PRECISE)
    moved = moved.reshape(field_count * tile_count, TILE, TILE)

    chosen = slot_labels(dest_slabs, peer_count, capacity)
    same_field = jnp.eye(field_count, dtype=jnp.bool_)
    picker = chosen.transpose(1, 2, 0, 3)[:, :, :, None, :] & same_field[None, None, :, :, None]
    picker = picker.astype(jnp.float32).reshape(
        peer_count, capacity, field_count, field_count * tile_count
    )
    packed = jnp.einsum("pcdk,kij->pcdij", picker, moved, precision=PRECISE)
    moved_tiles = lax.all_to_all(packed, "perp", split_axis=0, concat_axis=0, tiled=True)
    slot_target = jnp.sum(chosen.astype(jnp.int32) * (target[:, None, None, :] + 1), axis=3) - 1
    arrived_target = lax.all_to_all(
        slot_target.transpose(1, 2, 0), "perp", split_axis=0, concat_axis=0, tiled=True
    )

    position = jnp.arange(tile_count, dtype=jnp.int32)
    hit = arrived_target[None, None] == position[None, :, None, None, None]
    landing = hit & same_field[:, None, None, None, :]
    landing = landing.astype(jnp.float32).reshape(field_count, tile_count, -1)
    summed = jnp.einsum(
        "dtk,kij->dtij", landing, moved_tiles.reshape(-1, TILE, TILE), precision=PRECISE
    )
    deposit = join_tiles(summed, row_count, col_count)

    upward = [(i, i + 1) for i in range(plane_count - 1)]
    downward = [(i + 1, i) for i in range(plane_count - 1)]
    mapped = (
        lax.ppermute(deposit[0], "par", upward),
        lax.ppermute(deposit[1], "par", downward),
    )
    forward = [(i, i + 1) for i in range(peer_count - 1)]
    backward = [(i + 1, i) for i in range(peer_count - 1)]
    from_above = lax.ppermute(jnp.stack([m[-1:] for m in mapped]), "perp", forward)
    from_below = lax.ppermute(jnp.stack([m[:1] for m in mapped]), "perp", backward)
    chunk_rows = row_count // plane_count
    sides = []
    for f in range(field_count):
        smoothed = smooth_slab(mapped[f], from_above[f], from_below[f])
        side = local_pair[f] - smoothed
        if f == 1:
            side = -side
        sides.append(side.reshape(plane_count, chunk_rows, col_count))
    right_side = jnp.stack(sides, axis=1)
    lower, pivots, ratios = coefficients(band_terms)
    column_block = lax.all_to_all(right_side, "par", split_axis=0, concat_axis=0, tiled=True)
    solved = thomas(column_block, jnp.stack(lower), jnp.stack(pivots), jnp.stack(ratios))
    back = lax.all_to_all(solved, "par", split_axis=0, concat_axis=0, tiled=True)
    result = back.transpose(1, 0, 2, 3).reshape(field_count, 1, row_count, col_count)
    return result


def solution(mesh):
    placed = (
        P(None, "par", "perp", None),
        P(),
        P(None, "par", "perp", None),
        P(None, "par", "perp"),
        P(None, "par", "perp", None),
        P(),
    )
    return jax.shard_map(
        local, mesh=mesh, in_specs=placed, out_specs=P(None, "par", "perp", None), check_vma=False
    )
```

```python
import jax
import jax.numpy as jnp
from jax import lax
from jax.experimental import pallas as pl
from jax.experimental.pallas import tpu as pltpu
from jax.sharding import PartitionSpec as P

TILE = 128


PRECISE = lax.Precision.HIGHEST
KAPPA = 0.125


def split_tiles(plane_pair):
    field_count, row_count, col_count = plane_pair.shape
    shaped = plane_pair.reshape(field_count, row_count // TILE, TILE, col_count // TILE, TILE)
    return shaped.transpose(0, 1, 3, 2, 4).reshape(field_count, -1, TILE, TILE)


def join_tiles(tile_set, row_count, col_count):
    field_count = tile_set.shape[0]
    shaped = tile_set.reshape(field_count, row_count // TILE, col_count // TILE, TILE, TILE)
    return shaped.transpose(0, 1, 3, 2, 4).reshape(field_count, row_count, col_count)


def slot_labels(dest_slabs, peer_count, capacity):
    tile_count = dest_slabs.shape[-1]
    position = jnp.arange(tile_count, dtype=jnp.int32)
    earlier = position[:, None] > position[None, :]
    shared = dest_slabs[..., :, None] == dest_slabs[..., None, :]
    slot_rank = jnp.sum((shared & earlier).astype(jnp.int32), axis=-1)
    peer_ids = jnp.arange(peer_count, dtype=jnp.int32)
    slot_ids = jnp.arange(capacity, dtype=jnp.int32)
    chosen = (dest_slabs[..., None, None, :] == peer_ids[:, None, None]) & (
        slot_rank[..., None, None, :] == slot_ids[None, :, None]
    )
    return chosen


def thomas_kernel(band_ref, rhs_ref, out_ref, ratio_ref):
    depth = rhs_ref.shape[0]
    shape = rhs_ref.shape[1:]
    ratio = jnp.zeros(shape, jnp.float32)
    previous = jnp.zeros(shape, jnp.float32)
    for p in range(depth):
        lower_now = band_ref[0, p] if p > 0 else 0.0
        upper_now = band_ref[1, p] if p < depth - 1 else 0.0
        pivot = 1.0 - lower_now * ratio
        ratio = upper_now / pivot
        ratio_ref[p] = ratio
        previous = (rhs_ref[p] - lower_now * previous) / pivot
        out_ref[p] = previous
    following = previous
    for p in reversed(range(depth - 1)):
        following = out_ref[p] - ratio_ref[p] * following
        out_ref[p] = following


def thomas(rhs, band_terms):
    scalar = pl.BlockSpec(memory_space=pltpu.SMEM)
    whole = pl.BlockSpec(memory_space=pltpu.VMEM)
    return pl.pallas_call(
        thomas_kernel,
        out_shape=jax.ShapeDtypeStruct(rhs.shape, rhs.dtype),
        in_specs=[scalar, whole],
        out_specs=whole,
        scratch_shapes=[pltpu.VMEM(rhs.shape, jnp.float32)],
    )(band_terms, rhs)


def smooth_slab(plane, above_row, below_row):
    row_count, col_count = plane.shape
    zero_col = jnp.zeros((row_count, 1), plane.dtype)
    above = jnp.concatenate([above_row, plane[:-1]], axis=0)
    below = jnp.concatenate([plane[1:], below_row], axis=0)
    left = jnp.concatenate([zero_col, plane[:, :-1]], axis=1)
    right = jnp.concatenate([plane[:, 1:], zero_col], axis=1)
    beside_all = below + above + right + left
    return plane + KAPPA * (beside_all - 4.0 * plane)


def local(fields, weight_bank, dest_slab, dest_tile, tile_blocks, band_terms):
    peer_count = lax.axis_size("perp")
    plane_count = lax.axis_size("par")
    field_count, _, row_count, col_count = fields.shape
    local_pair = fields[:, 0]
    tile_set = split_tiles(local_pair)
    tile_count = tile_set.shape[1]
    capacity = max(2, (tile_count + peer_count - 1) // peer_count)
    dest_slabs = dest_slab[:, 0, :, 0]
    target = dest_tile[:, 0, :]
    left_index = tile_blocks[:, 0, :, 0]
    right_index = tile_blocks[:, 0, :, 1]

    left_block = jnp.take(weight_bank, left_index, axis=0, mode="clip")
    right_block = jnp.take(weight_bank, right_index, axis=0, mode="clip")
    shifted = jnp.einsum("dsij,dsjk->dsik", left_block, tile_set, precision=PRECISE)
    moved = jnp.einsum("dsik,dslk->dsil", shifted, right_block, precision=PRECISE)
    moved = moved.reshape(field_count * tile_count, TILE, TILE)

    chosen = slot_labels(dest_slabs, peer_count, capacity)
    same_field = jnp.eye(field_count, dtype=jnp.bool_)
    picker = chosen.transpose(1, 2, 0, 3)[:, :, :, None, :] & same_field[None, None, :, :, None]
    picker = picker.astype(jnp.float32).reshape(
        peer_count, capacity, field_count, field_count * tile_count
    )
    packed = jnp.einsum("pcdk,kij->pcdij", picker, moved, precision=PRECISE)
    moved_tiles = lax.all_to_all(packed, "perp", split_axis=0, concat_axis=0, tiled=True)
    slot_target = jnp.sum(chosen.astype(jnp.int32) * (target[:, None, None, :] + 1), axis=3) - 1
    arrived_target = lax.all_to_all(
        slot_target.transpose(1, 2, 0), "perp", split_axis=0, concat_axis=0, tiled=True
    )

    position = jnp.arange(tile_count, dtype=jnp.int32)
    hit = arrived_target[None, None] == position[None, :, None, None, None]
    landing = hit & same_field[:, None, None, None, :]
    landing = landing.astype(jnp.float32).reshape(field_count, tile_count, -1)
    summed = jnp.einsum(
        "dtk,kij->dtij", landing, moved_tiles.reshape(-1, TILE, TILE), precision=PRECISE
    )
    deposit = join_tiles(summed, row_count, col_count)

    upward = [(i, i + 1) for i in range(plane_count - 1)]
    downward = [(i + 1, i) for i in range(plane_count - 1)]
    mapped = (
        lax.ppermute(deposit[0], "par", upward),
        lax.ppermute(deposit[1], "par", downward),
    )

    def diagonal(plane_step, slab_step):
        pairs = []
        for p in range(plane_count):
            for j in range(peer_count):
                q, i = p - plane_step, j - slab_step
                if 0 <= q < plane_count and 0 <= i < peer_count:
                    pairs.append((q * peer_count + i, p * peer_count + j))
        return pairs

    from_above = [
        lax.ppermute(deposit[0, -1:], ("par", "perp"), diagonal(1, 1)),
        lax.ppermute(deposit[1, -1:], ("par", "perp"), diagonal(-1, 1)),
    ]
    from_below = [
        lax.ppermute(deposit[0, :1], ("par", "perp"), diagonal(1, -1)),
        lax.ppermute(deposit[1, :1], ("par", "perp"), diagonal(-1, -1)),
    ]
    chunk_rows = row_count // plane_count
    sides = []
    for f in range(field_count):
        smoothed = smooth_slab(mapped[f], from_above[f], from_below[f])
        side = local_pair[f] - smoothed
        if f == 1:
            side = -side
        sides.append(side.reshape(plane_count, chunk_rows, col_count))
    right_side = jnp.stack(sides, axis=1)
    column_block = lax.all_to_all(right_side, "par", split_axis=0, concat_axis=0, tiled=True)
    solved = thomas(column_block, band_terms)
    back = lax.all_to_all(solved, "par", split_axis=0, concat_axis=0, tiled=True)
    result = back.transpose(1, 0, 2, 3).reshape(field_count, 1, row_count, col_count)
    return result


def solution(mesh):
    placed = (
        P(None, "par", "perp", None),
        P(),
        P(None, "par", "perp", None),
        P(None, "par", "perp"),
        P(None, "par", "perp", None),
        P(),
    )
    return jax.shard_map(
        local, mesh=mesh, in_specs=placed, out_specs=P(None, "par", "perp", None), check_vma=False
    )
```

```python
import jax
import jax.numpy as jnp
from jax import lax
from jax.experimental import pallas as pl
from jax.experimental.pallas import tpu as pltpu
from jax.sharding import PartitionSpec as P

TILE = 128


PRECISE = lax.Precision.HIGHEST
KAPPA = 0.125


def split_tiles(plane_pair):
    field_count, row_count, col_count = plane_pair.shape
    shaped = plane_pair.reshape(field_count, row_count // TILE, TILE, col_count // TILE, TILE)
    return shaped.transpose(0, 1, 3, 2, 4).reshape(field_count, -1, TILE, TILE)


def join_tiles(tile_set, row_count, col_count):
    field_count = tile_set.shape[0]
    shaped = tile_set.reshape(field_count, row_count // TILE, col_count // TILE, TILE, TILE)
    return shaped.transpose(0, 1, 3, 2, 4).reshape(field_count, row_count, col_count)


def slot_labels(dest_slabs, peer_count, capacity):
    tile_count = dest_slabs.shape[-1]
    position = jnp.arange(tile_count, dtype=jnp.int32)
    earlier = position[:, None] > position[None, :]
    shared = dest_slabs[..., :, None] == dest_slabs[..., None, :]
    slot_rank = jnp.sum((shared & earlier).astype(jnp.int32), axis=-1)
    peer_ids = jnp.arange(peer_count, dtype=jnp.int32)
    slot_ids = jnp.arange(capacity, dtype=jnp.int32)
    chosen = (dest_slabs[..., None, None, :] == peer_ids[:, None, None]) & (
        slot_rank[..., None, None, :] == slot_ids[None, :, None]
    )
    return chosen


def thomas_kernel(band_ref, rhs_ref, out_ref, ratio_ref):
    depth = rhs_ref.shape[0]
    shape = rhs_ref.shape[1:]
    ratio = jnp.zeros(shape, jnp.float32)
    previous = jnp.zeros(shape, jnp.float32)
    for p in range(depth):
        lower_now = band_ref[0, p] if p > 0 else 0.0
        upper_now = band_ref[1, p] if p < depth - 1 else 0.0
        pivot = 1.0 - lower_now * ratio
        ratio = upper_now / pivot
        ratio_ref[p] = ratio
        previous = (rhs_ref[p] - lower_now * previous) / pivot
        out_ref[p] = previous
    following = previous
    for p in reversed(range(depth - 1)):
        following = out_ref[p] - ratio_ref[p] * following
        out_ref[p] = following


def thomas(rhs, band_terms):
    scalar = pl.BlockSpec(memory_space=pltpu.SMEM)
    whole = pl.BlockSpec(memory_space=pltpu.VMEM)
    return pl.pallas_call(
        thomas_kernel,
        out_shape=jax.ShapeDtypeStruct(rhs.shape, rhs.dtype),
        in_specs=[scalar, whole],
        out_specs=whole,
        scratch_shapes=[pltpu.VMEM(rhs.shape, jnp.float32)],
    )(band_terms, rhs)


def smooth_slab(plane, above_row, below_row):
    row_count, col_count = plane.shape
    zero_col = jnp.zeros((row_count, 1), plane.dtype)
    above = jnp.concatenate([above_row, plane[:-1]], axis=0)
    below = jnp.concatenate([plane[1:], below_row], axis=0)
    left = jnp.concatenate([zero_col, plane[:, :-1]], axis=1)
    right = jnp.concatenate([plane[:, 1:], zero_col], axis=1)
    beside_all = below + above + right + left
    return plane + KAPPA * (beside_all - 4.0 * plane)


def local(fields, weight_bank, dest_slab, dest_tile, tile_blocks, band_terms):
    peer_count = lax.axis_size("perp")
    plane_count = lax.axis_size("par")
    field_count, _, row_count, col_count = fields.shape
    local_pair = fields[:, 0]
    tile_set = split_tiles(local_pair)
    tile_count = tile_set.shape[1]
    capacity = max(2, (tile_count + peer_count - 1) // peer_count)
    dest_slabs = dest_slab[:, 0, :, 0]
    target = dest_tile[:, 0, :]
    left_index = tile_blocks[:, 0, :, 0]
    right_index = tile_blocks[:, 0, :, 1]

    left_block = jnp.take(weight_bank, left_index, axis=0, mode="clip")
    right_block = jnp.take(weight_bank, right_index, axis=0, mode="clip")
    shifted = jnp.einsum("dsij,dsjk->dsik", left_block, tile_set, precision=PRECISE)
    moved = jnp.einsum("dsik,dslk->dsil", shifted, right_block, precision=PRECISE)
    moved = moved.reshape(field_count * tile_count, TILE, TILE)

    chosen = slot_labels(dest_slabs, peer_count, capacity)
    same_field = jnp.eye(field_count, dtype=jnp.bool_)
    picker = chosen.transpose(1, 2, 0, 3)[:, :, :, None, :] & same_field[None, None, :, :, None]
    picker = picker.astype(jnp.float32).reshape(
        peer_count, capacity, field_count, field_count * tile_count
    )
    packed = jnp.einsum("pcdk,kij->pcdij", picker, moved, precision=PRECISE)
    moved_tiles = lax.all_to_all(packed, "perp", split_axis=0, concat_axis=0, tiled=True)
    slot_target = jnp.sum(chosen.astype(jnp.int32) * (target[:, None, None, :] + 1), axis=3) - 1
    arrived_target = lax.all_to_all(
        slot_target.transpose(1, 2, 0), "perp", split_axis=0, concat_axis=0, tiled=True
    )

    position = jnp.arange(tile_count, dtype=jnp.int32)
    hit = arrived_target[None, None] == position[None, :, None, None, None]
    landing = hit & same_field[:, None, None, None, :]
    landing = landing.astype(jnp.float32).reshape(field_count, tile_count, -1)
    summed = jnp.einsum(
        "dtk,kij->dtij", landing, moved_tiles.reshape(-1, TILE, TILE), precision=PRECISE
    )
    deposit = join_tiles(summed, row_count, col_count)

    upward = [(i, i + 1) for i in range(plane_count - 1)]
    downward = [(i + 1, i) for i in range(plane_count - 1)]
    mapped = (
        lax.ppermute(deposit[0], "par", upward),
        lax.ppermute(deposit[1], "par", downward),
    )

    forward = [(i, i + 1) for i in range(peer_count - 1)]
    backward = [(i + 1, i) for i in range(peer_count - 1)]
    from_above = lax.ppermute(jnp.stack([m[-1:] for m in mapped]), "perp", forward)
    from_below = lax.ppermute(jnp.stack([m[:1] for m in mapped]), "perp", backward)
    chunk_rows = row_count // plane_count
    sides = []
    for f in range(field_count):
        smoothed = smooth_slab(mapped[f], from_above[f], from_below[f])
        side = local_pair[f] - smoothed
        if f == 1:
            side = -side
        sides.append(side.reshape(plane_count, chunk_rows, col_count))
    right_side = jnp.stack(sides, axis=1)
    column_block = lax.all_to_all(right_side, "par", split_axis=0, concat_axis=0, tiled=True)
    solved = thomas(column_block, band_terms)
    back = lax.all_to_all(solved, "par", split_axis=0, concat_axis=0, tiled=True)
    result = back.transpose(1, 0, 2, 3).reshape(field_count, 1, row_count, col_count)
    return result


def solution(mesh):
    placed = (
        P(None, "par", "perp", None),
        P(),
        P(None, "par", "perp", None),
        P(None, "par", "perp"),
        P(None, "par", "perp", None),
        P(),
    )
    return jax.shard_map(
        local, mesh=mesh, in_specs=placed, out_specs=P(None, "par", "perp", None), check_vma=False
    )
```

```python
import jax
import jax.numpy as jnp
from jax import lax
from jax.experimental import pallas as pl
from jax.experimental.pallas import tpu as pltpu
from jax.sharding import PartitionSpec as P

TILE = 128


PRECISE = lax.Precision.HIGHEST
KAPPA = 0.125


def split_tiles(plane_pair):
    field_count, row_count, col_count = plane_pair.shape
    shaped = plane_pair.reshape(field_count, row_count // TILE, TILE, col_count // TILE, TILE)
    return shaped.transpose(0, 1, 3, 2, 4).reshape(field_count, -1, TILE, TILE)


def join_tiles(tile_set, row_count, col_count):
    field_count = tile_set.shape[0]
    shaped = tile_set.reshape(field_count, row_count // TILE, col_count // TILE, TILE, TILE)
    return shaped.transpose(0, 1, 3, 2, 4).reshape(field_count, row_count, col_count)


def slot_labels(dest_slabs, peer_count, capacity):
    tile_count = dest_slabs.shape[-1]
    position = jnp.arange(tile_count, dtype=jnp.int32)
    earlier = position[:, None] > position[None, :]
    shared = dest_slabs[..., :, None] == dest_slabs[..., None, :]
    slot_rank = jnp.sum((shared & earlier).astype(jnp.int32), axis=-1)
    peer_ids = jnp.arange(peer_count, dtype=jnp.int32)
    slot_ids = jnp.arange(capacity, dtype=jnp.int32)
    chosen = (dest_slabs[..., None, None, :] == peer_ids[:, None, None]) & (
        slot_rank[..., None, None, :] == slot_ids[None, :, None]
    )
    return chosen


def thomas_kernel(band_ref, rhs_ref, out_ref, ratio_ref):
    depth = rhs_ref.shape[0]
    shape = rhs_ref.shape[1:]
    ratio = jnp.zeros(shape, jnp.float32)
    previous = jnp.zeros(shape, jnp.float32)
    for p in range(depth):
        lower_now = band_ref[0, p] if p > 0 else 0.0
        upper_now = band_ref[1, p] if p < depth - 1 else 0.0
        pivot = 1.0 - lower_now * ratio
        ratio = upper_now / pivot
        ratio_ref[p] = ratio
        previous = (rhs_ref[p] - lower_now * previous) / pivot
        out_ref[p] = previous
    following = previous
    for p in reversed(range(depth - 1)):
        following = out_ref[p] - ratio_ref[p] * following
        out_ref[p] = following


def thomas(rhs, band_terms):
    scalar = pl.BlockSpec(memory_space=pltpu.SMEM)
    whole = pl.BlockSpec(memory_space=pltpu.VMEM)
    return pl.pallas_call(
        thomas_kernel,
        out_shape=jax.ShapeDtypeStruct(rhs.shape, rhs.dtype),
        in_specs=[scalar, whole],
        out_specs=whole,
        scratch_shapes=[pltpu.VMEM(rhs.shape, jnp.float32)],
    )(band_terms, rhs)


def smooth_slab(plane, above_row, below_row):
    row_count, col_count = plane.shape
    zero_col = jnp.zeros((row_count, 1), plane.dtype)
    above = jnp.concatenate([above_row, plane[:-1]], axis=0)
    below = jnp.concatenate([plane[1:], below_row], axis=0)
    left = jnp.concatenate([zero_col, plane[:, :-1]], axis=1)
    right = jnp.concatenate([plane[:, 1:], zero_col], axis=1)
    beside_all = below + above + right + left
    return plane + KAPPA * (beside_all - 4.0 * plane)


def local(fields, weight_bank, dest_slab, dest_tile, tile_blocks, band_terms):
    peer_count = lax.axis_size("perp")
    plane_count = lax.axis_size("par")
    field_count, _, row_count, col_count = fields.shape
    local_pair = fields[:, 0]
    upward = [(i, i + 1) for i in range(plane_count - 1)]
    downward = [(i + 1, i) for i in range(plane_count - 1)]
    indices = jnp.concatenate(
        [dest_slab[:, 0], dest_tile[:, 0, :, None], tile_blocks[:, 0]], axis=2
    )
    source_pair = jnp.stack(
        (
            lax.ppermute(local_pair[0], "par", upward),
            lax.ppermute(local_pair[1], "par", downward),
        )
    )
    source_indices = jnp.stack(
        (
            lax.ppermute(indices[0], "par", upward),
            lax.ppermute(indices[1], "par", downward),
        )
    )
    tile_set = split_tiles(source_pair)
    tile_count = tile_set.shape[1]
    capacity = max(2, (tile_count + peer_count - 1) // peer_count)
    dest_slabs = source_indices[:, :, 0]
    target = source_indices[:, :, 1]
    left_index = source_indices[:, :, 2]
    right_index = source_indices[:, :, 3]

    left_block = jnp.take(weight_bank, left_index, axis=0, mode="clip")
    right_block = jnp.take(weight_bank, right_index, axis=0, mode="clip")
    shifted = jnp.einsum("dsij,dsjk->dsik", left_block, tile_set, precision=PRECISE)
    moved = jnp.einsum("dsik,dslk->dsil", shifted, right_block, precision=PRECISE)
    moved = moved.reshape(field_count * tile_count, TILE, TILE)

    chosen = slot_labels(dest_slabs, peer_count, capacity)
    same_field = jnp.eye(field_count, dtype=jnp.bool_)
    picker = chosen.transpose(1, 2, 0, 3)[:, :, :, None, :] & same_field[None, None, :, :, None]
    picker = picker.astype(jnp.float32).reshape(
        peer_count, capacity, field_count, field_count * tile_count
    )
    packed = jnp.einsum("pcdk,kij->pcdij", picker, moved, precision=PRECISE)
    moved_tiles = lax.all_to_all(packed, "perp", split_axis=0, concat_axis=0, tiled=True)
    slot_target = jnp.sum(chosen.astype(jnp.int32) * (target[:, None, None, :] + 1), axis=3) - 1
    arrived_target = lax.all_to_all(
        slot_target.transpose(1, 2, 0), "perp", split_axis=0, concat_axis=0, tiled=True
    )

    position = jnp.arange(tile_count, dtype=jnp.int32)
    hit = arrived_target[None, None] == position[None, :, None, None, None]
    landing = hit & same_field[:, None, None, None, :]
    landing = landing.astype(jnp.float32).reshape(field_count, tile_count, -1)
    summed = jnp.einsum(
        "dtk,kij->dtij", landing, moved_tiles.reshape(-1, TILE, TILE), precision=PRECISE
    )
    deposit = join_tiles(summed, row_count, col_count)

    mapped = (deposit[0], deposit[1])
    forward = [(i, i + 1) for i in range(peer_count - 1)]
    backward = [(i + 1, i) for i in range(peer_count - 1)]
    from_above = lax.ppermute(jnp.stack([m[-1:] for m in mapped]), "perp", forward)
    from_below = lax.ppermute(jnp.stack([m[:1] for m in mapped]), "perp", backward)
    chunk_rows = row_count // plane_count
    sides = []
    for f in range(field_count):
        smoothed = smooth_slab(mapped[f], from_above[f], from_below[f])
        side = local_pair[f] - smoothed
        if f == 1:
            side = -side
        sides.append(side.reshape(plane_count, chunk_rows, col_count))
    right_side = jnp.stack(sides, axis=1)
    column_block = lax.all_to_all(right_side, "par", split_axis=0, concat_axis=0, tiled=True)
    solved = thomas(column_block, band_terms)
    back = lax.all_to_all(solved, "par", split_axis=0, concat_axis=0, tiled=True)
    result = back.transpose(1, 0, 2, 3).reshape(field_count, 1, row_count, col_count)
    return result


def solution(mesh):
    placed = (
        P(None, "par", "perp", None),
        P(),
        P(None, "par", "perp", None),
        P(None, "par", "perp"),
        P(None, "par", "perp", None),
        P(),
    )
    return jax.shard_map(
        local, mesh=mesh, in_specs=placed, out_specs=P(None, "par", "perp", None), check_vma=False
    )
```

```python
import jax
import jax.numpy as jnp
from jax import lax
from jax.experimental import pallas as pl
from jax.experimental.pallas import tpu as pltpu
from jax.sharding import PartitionSpec as P

TILE = 128


PRECISE = lax.Precision.HIGHEST
THREE_PASS = lax.Precision.HIGH
KAPPA = 0.125


def split_tiles(plane_pair):
    field_count, row_count, col_count = plane_pair.shape
    shaped = plane_pair.reshape(field_count, row_count // TILE, TILE, col_count // TILE, TILE)
    return shaped.transpose(0, 1, 3, 2, 4).reshape(field_count, -1, TILE, TILE)


def join_tiles(tile_set, row_count, col_count):
    field_count = tile_set.shape[0]
    shaped = tile_set.reshape(field_count, row_count // TILE, col_count // TILE, TILE, TILE)
    return shaped.transpose(0, 1, 3, 2, 4).reshape(field_count, row_count, col_count)


def slot_labels(dest_slabs, peer_count, capacity):
    tile_count = dest_slabs.shape[-1]
    position = jnp.arange(tile_count, dtype=jnp.int32)
    earlier = position[:, None] > position[None, :]
    shared = dest_slabs[..., :, None] == dest_slabs[..., None, :]
    slot_rank = jnp.sum((shared & earlier).astype(jnp.int32), axis=-1)
    peer_ids = jnp.arange(peer_count, dtype=jnp.int32)
    slot_ids = jnp.arange(capacity, dtype=jnp.int32)
    chosen = (dest_slabs[..., None, None, :] == peer_ids[:, None, None]) & (
        slot_rank[..., None, None, :] == slot_ids[None, :, None]
    )
    return chosen


def thomas_kernel(band_ref, rhs_ref, out_ref, ratio_ref):
    depth = rhs_ref.shape[0]
    shape = rhs_ref.shape[1:]
    ratio = jnp.zeros(shape, jnp.float32)
    previous = jnp.zeros(shape, jnp.float32)
    for p in range(depth):
        lower_now = band_ref[0, p] if p > 0 else 0.0
        upper_now = band_ref[1, p] if p < depth - 1 else 0.0
        pivot = 1.0 - lower_now * ratio
        ratio = upper_now / pivot
        ratio_ref[p] = ratio
        previous = (rhs_ref[p] - lower_now * previous) / pivot
        out_ref[p] = previous
    following = previous
    for p in reversed(range(depth - 1)):
        following = out_ref[p] - ratio_ref[p] * following
        out_ref[p] = following


def thomas(rhs, band_terms):
    scalar = pl.BlockSpec(memory_space=pltpu.SMEM)
    whole = pl.BlockSpec(memory_space=pltpu.VMEM)
    return pl.pallas_call(
        thomas_kernel,
        out_shape=jax.ShapeDtypeStruct(rhs.shape, rhs.dtype),
        in_specs=[scalar, whole],
        out_specs=whole,
        scratch_shapes=[pltpu.VMEM(rhs.shape, jnp.float32)],
    )(band_terms, rhs)


def smooth_slab(plane, above_row, below_row):
    row_count, col_count = plane.shape
    zero_col = jnp.zeros((row_count, 1), plane.dtype)
    above = jnp.concatenate([above_row, plane[:-1]], axis=0)
    below = jnp.concatenate([plane[1:], below_row], axis=0)
    left = jnp.concatenate([zero_col, plane[:, :-1]], axis=1)
    right = jnp.concatenate([plane[:, 1:], zero_col], axis=1)
    beside_all = below + above + right + left
    return plane + KAPPA * (beside_all - 4.0 * plane)


def local(fields, weight_bank, dest_slab, dest_tile, tile_blocks, band_terms):
    peer_count = lax.axis_size("perp")
    plane_count = lax.axis_size("par")
    field_count, _, row_count, col_count = fields.shape
    local_pair = fields[:, 0]
    tile_set = split_tiles(local_pair)
    tile_count = tile_set.shape[1]
    capacity = max(2, (tile_count + peer_count - 1) // peer_count)
    dest_slabs = dest_slab[:, 0, :, 0]
    target = dest_tile[:, 0, :]
    left_index = tile_blocks[:, 0, :, 0]
    right_index = tile_blocks[:, 0, :, 1]

    left_block = jnp.take(weight_bank, left_index, axis=0, mode="clip")
    right_block = jnp.take(weight_bank, right_index, axis=0, mode="clip")
    shifted = jnp.einsum("dsij,dsjk->dsik", left_block, tile_set, precision=THREE_PASS)
    moved = jnp.einsum("dsik,dslk->dsil", shifted, right_block, precision=THREE_PASS)
    moved = moved.reshape(field_count * tile_count, TILE, TILE)

    chosen = slot_labels(dest_slabs, peer_count, capacity)
    same_field = jnp.eye(field_count, dtype=jnp.bool_)
    picker = chosen.transpose(1, 2, 0, 3)[:, :, :, None, :] & same_field[None, None, :, :, None]
    picker = picker.astype(jnp.float32).reshape(
        peer_count, capacity, field_count, field_count * tile_count
    )
    packed = jnp.einsum("pcdk,kij->pcdij", picker, moved, precision=THREE_PASS)
    moved_tiles = lax.all_to_all(packed, "perp", split_axis=0, concat_axis=0, tiled=True)
    slot_target = jnp.sum(chosen.astype(jnp.int32) * (target[:, None, None, :] + 1), axis=3) - 1
    arrived_target = lax.all_to_all(
        slot_target.transpose(1, 2, 0), "perp", split_axis=0, concat_axis=0, tiled=True
    )

    position = jnp.arange(tile_count, dtype=jnp.int32)
    hit = arrived_target[None, None] == position[None, :, None, None, None]
    landing = hit & same_field[:, None, None, None, :]
    landing = landing.astype(jnp.float32).reshape(field_count, tile_count, -1)
    summed = jnp.einsum(
        "dtk,kij->dtij", landing, moved_tiles.reshape(-1, TILE, TILE), precision=THREE_PASS
    )
    deposit = join_tiles(summed, row_count, col_count)

    upward = [(i, i + 1) for i in range(plane_count - 1)]
    downward = [(i + 1, i) for i in range(plane_count - 1)]
    mapped = (
        lax.ppermute(deposit[0], "par", upward),
        lax.ppermute(deposit[1], "par", downward),
    )

    forward = [(i, i + 1) for i in range(peer_count - 1)]
    backward = [(i + 1, i) for i in range(peer_count - 1)]
    from_above = lax.ppermute(jnp.stack([m[-1:] for m in mapped]), "perp", forward)
    from_below = lax.ppermute(jnp.stack([m[:1] for m in mapped]), "perp", backward)
    chunk_rows = row_count // plane_count
    sides = []
    for f in range(field_count):
        smoothed = smooth_slab(mapped[f], from_above[f], from_below[f])
        side = local_pair[f] - smoothed
        if f == 1:
            side = -side
        sides.append(side.reshape(plane_count, chunk_rows, col_count))
    right_side = jnp.stack(sides, axis=1)
    column_block = lax.all_to_all(right_side, "par", split_axis=0, concat_axis=0, tiled=True)
    solved = thomas(column_block, band_terms)
    back = lax.all_to_all(solved, "par", split_axis=0, concat_axis=0, tiled=True)
    result = back.transpose(1, 0, 2, 3).reshape(field_count, 1, row_count, col_count)
    return result


def solution(mesh):
    placed = (
        P(None, "par", "perp", None),
        P(),
        P(None, "par", "perp", None),
        P(None, "par", "perp"),
        P(None, "par", "perp", None),
        P(),
    )
    return jax.shard_map(
        local, mesh=mesh, in_specs=placed, out_specs=P(None, "par", "perp", None), check_vma=False
    )
```

```python
import jax
import jax.numpy as jnp
from jax import lax
from jax.experimental import pallas as pl
from jax.experimental.pallas import tpu as pltpu
from jax.sharding import PartitionSpec as P

TILE = 128


PRECISE = lax.Precision.HIGHEST
THREE_PASS = lax.Precision.HIGH
KAPPA = 0.125


def split_tiles(plane_pair):
    field_count, row_count, col_count = plane_pair.shape
    shaped = plane_pair.reshape(field_count, row_count // TILE, TILE, col_count // TILE, TILE)
    return shaped.transpose(0, 1, 3, 2, 4).reshape(field_count, -1, TILE, TILE)


def join_tiles(tile_set, row_count, col_count):
    field_count = tile_set.shape[0]
    shaped = tile_set.reshape(field_count, row_count // TILE, col_count // TILE, TILE, TILE)
    return shaped.transpose(0, 1, 3, 2, 4).reshape(field_count, row_count, col_count)


def slot_labels(dest_slabs, peer_count, capacity):
    tile_count = dest_slabs.shape[-1]
    position = jnp.arange(tile_count, dtype=jnp.int32)
    earlier = position[:, None] > position[None, :]
    shared = dest_slabs[..., :, None] == dest_slabs[..., None, :]
    slot_rank = jnp.sum((shared & earlier).astype(jnp.int32), axis=-1)
    peer_ids = jnp.arange(peer_count, dtype=jnp.int32)
    slot_ids = jnp.arange(capacity, dtype=jnp.int32)
    chosen = (dest_slabs[..., None, None, :] == peer_ids[:, None, None]) & (
        slot_rank[..., None, None, :] == slot_ids[None, :, None]
    )
    return chosen


def thomas_kernel(band_ref, rhs_ref, out_ref, ratio_ref):
    depth = rhs_ref.shape[0]
    shape = rhs_ref.shape[1:]
    ratio = jnp.zeros(shape, jnp.float32)
    previous = jnp.zeros(shape, jnp.float32)
    for p in range(depth):
        lower_now = band_ref[0, p] if p > 0 else 0.0
        upper_now = band_ref[1, p] if p < depth - 1 else 0.0
        pivot = 1.0 - lower_now * ratio
        ratio = upper_now / pivot
        ratio_ref[p] = ratio
        previous = (rhs_ref[p] - lower_now * previous) / pivot
        out_ref[p] = previous
    following = previous
    for p in reversed(range(depth - 1)):
        following = out_ref[p] - ratio_ref[p] * following
        out_ref[p] = following


def thomas(rhs, band_terms):
    scalar = pl.BlockSpec(memory_space=pltpu.SMEM)
    whole = pl.BlockSpec(memory_space=pltpu.VMEM)
    return pl.pallas_call(
        thomas_kernel,
        out_shape=jax.ShapeDtypeStruct(rhs.shape, rhs.dtype),
        in_specs=[scalar, whole],
        out_specs=whole,
        scratch_shapes=[pltpu.VMEM(rhs.shape, jnp.float32)],
    )(band_terms, rhs)


def landing_kernel(label_ref, recv_ref, out_ref, acc_ref):
    field_count = out_ref.shape[0]
    tiles_across = out_ref.shape[2] // TILE
    acc_ref[...] = jnp.zeros(acc_ref.shape, jnp.float32)
    for k in range(recv_ref.shape[0]):
        field = k % field_count
        label = label_ref[k]
        acc_ref[field, label] = acc_ref[field, label] + recv_ref[k]
    for field in range(field_count):
        for t in range(acc_ref.shape[1] - 1):
            a, b = divmod(t, tiles_across)
            out_ref[field, a * TILE:(a + 1) * TILE, b * TILE:(b + 1) * TILE] = acc_ref[field, t + 1]


def land(labels, received, field_count, tile_count, row_count, col_count):
    scalar = pl.BlockSpec(memory_space=pltpu.SMEM)
    whole = pl.BlockSpec(memory_space=pltpu.VMEM)
    return pl.pallas_call(
        landing_kernel,
        out_shape=jax.ShapeDtypeStruct((field_count, row_count, col_count), received.dtype),
        in_specs=[scalar, whole],
        out_specs=whole,
        scratch_shapes=[pltpu.VMEM((field_count, tile_count + 1, TILE, TILE), jnp.float32)],
    )(labels, received)


def smooth_slab(plane, above_row, below_row):
    row_count, col_count = plane.shape
    zero_col = jnp.zeros((row_count, 1), plane.dtype)
    above = jnp.concatenate([above_row, plane[:-1]], axis=0)
    below = jnp.concatenate([plane[1:], below_row], axis=0)
    left = jnp.concatenate([zero_col, plane[:, :-1]], axis=1)
    right = jnp.concatenate([plane[:, 1:], zero_col], axis=1)
    beside_all = below + above + right + left
    return plane + KAPPA * (beside_all - 4.0 * plane)


def local(fields, weight_bank, dest_slab, dest_tile, tile_blocks, band_terms):
    peer_count = lax.axis_size("perp")
    plane_count = lax.axis_size("par")
    field_count, _, row_count, col_count = fields.shape
    local_pair = fields[:, 0]
    tile_set = split_tiles(local_pair)
    tile_count = tile_set.shape[1]
    capacity = max(2, (tile_count + peer_count - 1) // peer_count)
    dest_slabs = dest_slab[:, 0, :, 0]
    target = dest_tile[:, 0, :]
    left_index = tile_blocks[:, 0, :, 0]
    right_index = tile_blocks[:, 0, :, 1]

    left_block = jnp.take(weight_bank, left_index, axis=0, mode="clip")
    right_block = jnp.take(weight_bank, right_index, axis=0, mode="clip")
    shifted = jnp.einsum("dsij,dsjk->dsik", left_block, tile_set, precision=THREE_PASS)
    moved = jnp.einsum("dsik,dslk->dsil", shifted, right_block, precision=THREE_PASS)
    moved = moved.reshape(field_count * tile_count, TILE, TILE)

    chosen = slot_labels(dest_slabs, peer_count, capacity)
    same_field = jnp.eye(field_count, dtype=jnp.bool_)
    picker = chosen.transpose(1, 2, 0, 3)[:, :, :, None, :] & same_field[None, None, :, :, None]
    picker = picker.astype(jnp.float32).reshape(
        peer_count, capacity, field_count, field_count * tile_count
    )
    packed = jnp.einsum("pcdk,kij->pcdij", picker, moved, precision=THREE_PASS)
    moved_tiles = lax.all_to_all(packed, "perp", split_axis=0, concat_axis=0, tiled=True)
    slot_target = jnp.sum(chosen.astype(jnp.int32) * (target[:, None, None, :] + 1), axis=3) - 1
    arrived_target = lax.all_to_all(
        slot_target.transpose(1, 2, 0), "perp", split_axis=0, concat_axis=0, tiled=True
    )

    labels = jnp.clip(arrived_target.reshape(-1) + 1, 0, tile_count)
    deposit = land(
        labels, moved_tiles.reshape(-1, TILE, TILE), field_count, tile_count, row_count, col_count
    )

    upward = [(i, i + 1) for i in range(plane_count - 1)]
    downward = [(i + 1, i) for i in range(plane_count - 1)]
    mapped = (
        lax.ppermute(deposit[0], "par", upward),
        lax.ppermute(deposit[1], "par", downward),
    )

    forward = [(i, i + 1) for i in range(peer_count - 1)]
    backward = [(i + 1, i) for i in range(peer_count - 1)]
    from_above = lax.ppermute(jnp.stack([m[-1:] for m in mapped]), "perp", forward)
    from_below = lax.ppermute(jnp.stack([m[:1] for m in mapped]), "perp", backward)
    chunk_rows = row_count // plane_count
    sides = []
    for f in range(field_count):
        smoothed = smooth_slab(mapped[f], from_above[f], from_below[f])
        side = local_pair[f] - smoothed
        if f == 1:
            side = -side
        sides.append(side.reshape(plane_count, chunk_rows, col_count))
    right_side = jnp.stack(sides, axis=1)
    column_block = lax.all_to_all(right_side, "par", split_axis=0, concat_axis=0, tiled=True)
    solved = thomas(column_block, band_terms)
    back = lax.all_to_all(solved, "par", split_axis=0, concat_axis=0, tiled=True)
    result = back.transpose(1, 0, 2, 3).reshape(field_count, 1, row_count, col_count)
    return result


def solution(mesh):
    placed = (
        P(None, "par", "perp", None),
        P(),
        P(None, "par", "perp", None),
        P(None, "par", "perp"),
        P(None, "par", "perp", None),
        P(),
    )
    return jax.shard_map(
        local, mesh=mesh, in_specs=placed, out_specs=P(None, "par", "perp", None), check_vma=False
    )
```

```python
import jax
import jax.numpy as jnp
from jax import lax
from jax.experimental import pallas as pl
from jax.experimental.pallas import tpu as pltpu
from jax.sharding import PartitionSpec as P

TILE = 128


PRECISE = lax.Precision.HIGHEST
THREE_PASS = lax.Precision.HIGH
KAPPA = 0.125


def split_tiles(plane_pair):
    field_count, row_count, col_count = plane_pair.shape
    shaped = plane_pair.reshape(field_count, row_count // TILE, TILE, col_count // TILE, TILE)
    return shaped.transpose(0, 1, 3, 2, 4).reshape(field_count, -1, TILE, TILE)


def join_tiles(tile_set, row_count, col_count):
    field_count = tile_set.shape[0]
    shaped = tile_set.reshape(field_count, row_count // TILE, col_count // TILE, TILE, TILE)
    return shaped.transpose(0, 1, 3, 2, 4).reshape(field_count, row_count, col_count)


def slot_labels(dest_slabs, peer_count, capacity):
    tile_count = dest_slabs.shape[-1]
    position = jnp.arange(tile_count, dtype=jnp.int32)
    earlier = position[:, None] > position[None, :]
    shared = dest_slabs[..., :, None] == dest_slabs[..., None, :]
    slot_rank = jnp.sum((shared & earlier).astype(jnp.int32), axis=-1)
    peer_ids = jnp.arange(peer_count, dtype=jnp.int32)
    slot_ids = jnp.arange(capacity, dtype=jnp.int32)
    chosen = (dest_slabs[..., None, None, :] == peer_ids[:, None, None]) & (
        slot_rank[..., None, None, :] == slot_ids[None, :, None]
    )
    return chosen


def thomas_kernel(band_ref, rhs_ref, out_ref, ratio_ref):
    depth = rhs_ref.shape[0]
    shape = rhs_ref.shape[1:]
    ratio = jnp.zeros(shape, jnp.float32)
    previous = jnp.zeros(shape, jnp.float32)
    for p in range(depth):
        lower_now = band_ref[0, p] if p > 0 else 0.0
        upper_now = band_ref[1, p] if p < depth - 1 else 0.0
        pivot = 1.0 - lower_now * ratio
        ratio = upper_now / pivot
        ratio_ref[p] = ratio
        previous = (rhs_ref[p] - lower_now * previous) / pivot
        out_ref[p] = previous
    following = previous
    for p in reversed(range(depth - 1)):
        following = out_ref[p] - ratio_ref[p] * following
        out_ref[p] = following


def thomas(rhs, band_terms):
    scalar = pl.BlockSpec(memory_space=pltpu.SMEM)
    whole = pl.BlockSpec(memory_space=pltpu.VMEM)
    return pl.pallas_call(
        thomas_kernel,
        out_shape=jax.ShapeDtypeStruct(rhs.shape, rhs.dtype),
        in_specs=[scalar, whole],
        out_specs=whole,
        scratch_shapes=[pltpu.VMEM(rhs.shape, jnp.float32)],
    )(band_terms, rhs)


def landing_kernel(label_ref, recv_ref, out_ref, acc_ref):
    field_count = out_ref.shape[0]
    tiles_across = out_ref.shape[2] // TILE
    acc_ref[...] = jnp.zeros(acc_ref.shape, jnp.float32)
    for k in range(recv_ref.shape[0]):
        field = k % field_count
        label = label_ref[k]
        acc_ref[field, label] = acc_ref[field, label] + recv_ref[k]
    for field in range(field_count):
        for t in range(acc_ref.shape[1] - 1):
            a, b = divmod(t, tiles_across)
            out_ref[field, a * TILE:(a + 1) * TILE, b * TILE:(b + 1) * TILE] = acc_ref[field, t + 1]


def land(labels, received, field_count, tile_count, row_count, col_count):
    scalar = pl.BlockSpec(memory_space=pltpu.SMEM)
    whole = pl.BlockSpec(memory_space=pltpu.VMEM)
    return pl.pallas_call(
        landing_kernel,
        out_shape=jax.ShapeDtypeStruct((field_count, row_count, col_count), received.dtype),
        in_specs=[scalar, whole],
        out_specs=whole,
        scratch_shapes=[pltpu.VMEM((field_count, tile_count + 1, TILE, TILE), jnp.float32)],
    )(labels, received)


def smooth_slab(plane, above_row, below_row):
    row_count, col_count = plane.shape
    zero_col = jnp.zeros((row_count, 1), plane.dtype)
    above = jnp.concatenate([above_row, plane[:-1]], axis=0)
    below = jnp.concatenate([plane[1:], below_row], axis=0)
    left = jnp.concatenate([zero_col, plane[:, :-1]], axis=1)
    right = jnp.concatenate([plane[:, 1:], zero_col], axis=1)
    beside_all = below + above + right + left
    return plane + KAPPA * (beside_all - 4.0 * plane)


def local(fields, weight_bank, dest_slab, dest_tile, tile_blocks, band_terms):
    peer_count = lax.axis_size("perp")
    plane_count = lax.axis_size("par")
    field_count, _, row_count, col_count = fields.shape
    local_pair = fields[:, 0]
    tile_set = split_tiles(local_pair)
    tile_count = tile_set.shape[1]
    capacity = max(2, (tile_count + peer_count - 1) // peer_count)
    dest_slabs = dest_slab[:, 0, :, 0]
    target = dest_tile[:, 0, :]
    left_index = tile_blocks[:, 0, :, 0]
    right_index = tile_blocks[:, 0, :, 1]

    left_block = jnp.take(weight_bank, left_index, axis=0, mode="clip")
    right_block = jnp.take(weight_bank, right_index, axis=0, mode="clip")
    shifted = jnp.einsum("dsij,dsjk->dsik", left_block, tile_set, precision=THREE_PASS)
    moved = jnp.einsum("dsik,dslk->dsil", shifted, right_block, precision=THREE_PASS)
    moved = moved.reshape(field_count * tile_count, TILE, TILE)

    chosen = slot_labels(dest_slabs, peer_count, capacity)
    tile_ids = (
        jnp.arange(field_count, dtype=jnp.int32)[:, None] * tile_count
        + jnp.arange(tile_count, dtype=jnp.int32)[None, :]
    )
    source_id = jnp.sum(chosen.astype(jnp.int32) * (tile_ids[:, None, None, :] + 1), axis=3) - 1
    source_id = jnp.where(source_id < 0, field_count * tile_count, source_id)
    with_blank = jnp.concatenate([moved, jnp.zeros((1, TILE, TILE), moved.dtype)], axis=0)
    packed = jnp.take(with_blank, source_id.transpose(1, 2, 0), axis=0, mode="clip")
    moved_tiles = lax.all_to_all(packed, "perp", split_axis=0, concat_axis=0, tiled=True)
    slot_target = jnp.sum(chosen.astype(jnp.int32) * (target[:, None, None, :] + 1), axis=3) - 1
    arrived_target = lax.all_to_all(
        slot_target.transpose(1, 2, 0), "perp", split_axis=0, concat_axis=0, tiled=True
    )

    labels = jnp.clip(arrived_target.reshape(-1) + 1, 0, tile_count)
    deposit = land(
        labels, moved_tiles.reshape(-1, TILE, TILE), field_count, tile_count, row_count, col_count
    )

    upward = [(i, i + 1) for i in range(plane_count - 1)]
    downward = [(i + 1, i) for i in range(plane_count - 1)]
    mapped = (
        lax.ppermute(deposit[0], "par", upward),
        lax.ppermute(deposit[1], "par", downward),
    )

    forward = [(i, i + 1) for i in range(peer_count - 1)]
    backward = [(i + 1, i) for i in range(peer_count - 1)]
    from_above = lax.ppermute(jnp.stack([m[-1:] for m in mapped]), "perp", forward)
    from_below = lax.ppermute(jnp.stack([m[:1] for m in mapped]), "perp", backward)
    chunk_rows = row_count // plane_count
    sides = []
    for f in range(field_count):
        smoothed = smooth_slab(mapped[f], from_above[f], from_below[f])
        side = local_pair[f] - smoothed
        if f == 1:
            side = -side
        sides.append(side.reshape(plane_count, chunk_rows, col_count))
    right_side = jnp.stack(sides, axis=1)
    column_block = lax.all_to_all(right_side, "par", split_axis=0, concat_axis=0, tiled=True)
    solved = thomas(column_block, band_terms)
    back = lax.all_to_all(solved, "par", split_axis=0, concat_axis=0, tiled=True)
    result = back.transpose(1, 0, 2, 3).reshape(field_count, 1, row_count, col_count)
    return result


def solution(mesh):
    placed = (
        P(None, "par", "perp", None),
        P(),
        P(None, "par", "perp", None),
        P(None, "par", "perp"),
        P(None, "par", "perp", None),
        P(),
    )
    return jax.shard_map(
        local, mesh=mesh, in_specs=placed, out_specs=P(None, "par", "perp", None), check_vma=False
    )
```

```python
import jax
import jax.numpy as jnp
from jax import lax
from jax.experimental import pallas as pl
from jax.experimental.pallas import tpu as pltpu
from jax.sharding import PartitionSpec as P

TILE = 128


PRECISE = lax.Precision.HIGHEST
THREE_PASS = lax.Precision.HIGH
KAPPA = 0.125


def split_tiles(plane_pair):
    field_count, row_count, col_count = plane_pair.shape
    shaped = plane_pair.reshape(field_count, row_count // TILE, TILE, col_count // TILE, TILE)
    return shaped.transpose(0, 1, 3, 2, 4).reshape(field_count, -1, TILE, TILE)


def join_tiles(tile_set, row_count, col_count):
    field_count = tile_set.shape[0]
    shaped = tile_set.reshape(field_count, row_count // TILE, col_count // TILE, TILE, TILE)
    return shaped.transpose(0, 1, 3, 2, 4).reshape(field_count, row_count, col_count)


def slot_labels(dest_slabs, peer_count, capacity):
    tile_count = dest_slabs.shape[-1]
    position = jnp.arange(tile_count, dtype=jnp.int32)
    earlier = position[:, None] > position[None, :]
    shared = dest_slabs[..., :, None] == dest_slabs[..., None, :]
    slot_rank = jnp.sum((shared & earlier).astype(jnp.int32), axis=-1)
    peer_ids = jnp.arange(peer_count, dtype=jnp.int32)
    slot_ids = jnp.arange(capacity, dtype=jnp.int32)
    chosen = (dest_slabs[..., None, None, :] == peer_ids[:, None, None]) & (
        slot_rank[..., None, None, :] == slot_ids[None, :, None]
    )
    return chosen


def thomas_kernel(band_ref, rhs_ref, out_ref, ratio_ref):
    depth = rhs_ref.shape[0]
    shape = rhs_ref.shape[1:]
    ratio = jnp.zeros(shape, jnp.float32)
    previous = jnp.zeros(shape, jnp.float32)
    for p in range(depth):
        lower_now = band_ref[0, p] if p > 0 else 0.0
        upper_now = band_ref[1, p] if p < depth - 1 else 0.0
        pivot = 1.0 - lower_now * ratio
        ratio = upper_now / pivot
        ratio_ref[p] = ratio
        previous = (rhs_ref[p] - lower_now * previous) / pivot
        out_ref[p] = previous
    following = previous
    for p in reversed(range(depth - 1)):
        following = out_ref[p] - ratio_ref[p] * following
        out_ref[p] = following


def thomas(rhs, band_terms):
    scalar = pl.BlockSpec(memory_space=pltpu.SMEM)
    whole = pl.BlockSpec(memory_space=pltpu.VMEM)
    return pl.pallas_call(
        thomas_kernel,
        out_shape=jax.ShapeDtypeStruct(rhs.shape, rhs.dtype),
        in_specs=[scalar, whole],
        out_specs=whole,
        scratch_shapes=[pltpu.VMEM(rhs.shape, jnp.float32)],
    )(band_terms, rhs)


def moving_kernel(source_ref, block_ref, plane_ref, bank_ref, out_ref, moved_ref):
    field_count = plane_ref.shape[0]
    tiles_across = plane_ref.shape[2] // TILE
    tile_count = (plane_ref.shape[1] // TILE) * tiles_across
    blank = field_count * tile_count
    moved_ref[blank] = jnp.zeros((TILE, TILE), jnp.float32)
    for field in range(field_count):
        for s in range(tile_count):
            a, b = divmod(s, tiles_across)
            tile = plane_ref[field, a * TILE:(a + 1) * TILE, b * TILE:(b + 1) * TILE]
            left = bank_ref[block_ref[0, field * tile_count + s]]
            right = bank_ref[block_ref[1, field * tile_count + s]]
            shifted = jnp.dot(left, tile, precision=PRECISE, preferred_element_type=jnp.float32)
            moved_ref[field * tile_count + s] = lax.dot_general(
                shifted, right, (((1,), (1,)), ((), ())),
                precision=PRECISE, preferred_element_type=jnp.float32,
            )
    for k in range(out_ref.shape[0]):
        out_ref[k] = moved_ref[source_ref[k]]


def move_and_pack(source_ids, blocks, planes, weight_bank, slot_count):
    scalar = pl.BlockSpec(memory_space=pltpu.SMEM)
    whole = pl.BlockSpec(memory_space=pltpu.VMEM)
    field_count, row_count, col_count = planes.shape
    tile_total = field_count * (row_count // TILE) * (col_count // TILE)
    return pl.pallas_call(
        moving_kernel,
        out_shape=jax.ShapeDtypeStruct((slot_count, TILE, TILE), planes.dtype),
        in_specs=[scalar, scalar, whole, whole],
        out_specs=whole,
        scratch_shapes=[pltpu.VMEM((tile_total + 1, TILE, TILE), jnp.float32)],
    )(source_ids, blocks, planes, weight_bank)


def landing_kernel(label_ref, recv_ref, out_ref, acc_ref):
    field_count = out_ref.shape[0]
    tiles_across = out_ref.shape[2] // TILE
    acc_ref[...] = jnp.zeros(acc_ref.shape, jnp.float32)
    for k in range(recv_ref.shape[0]):
        field = k % field_count
        label = label_ref[k]
        acc_ref[field, label] = acc_ref[field, label] + recv_ref[k]
    for field in range(field_count):
        for t in range(acc_ref.shape[1] - 1):
            a, b = divmod(t, tiles_across)
            out_ref[field, a * TILE:(a + 1) * TILE, b * TILE:(b + 1) * TILE] = acc_ref[field, t + 1]


def land(labels, received, field_count, tile_count, row_count, col_count):
    scalar = pl.BlockSpec(memory_space=pltpu.SMEM)
    whole = pl.BlockSpec(memory_space=pltpu.VMEM)
    return pl.pallas_call(
        landing_kernel,
        out_shape=jax.ShapeDtypeStruct((field_count, row_count, col_count), received.dtype),
        in_specs=[scalar, whole],
        out_specs=whole,
        scratch_shapes=[pltpu.VMEM((field_count, tile_count + 1, TILE, TILE), jnp.float32)],
    )(labels, received)


def smooth_slab(plane, above_row, below_row):
    row_count, col_count = plane.shape
    zero_col = jnp.zeros((row_count, 1), plane.dtype)
    above = jnp.concatenate([above_row, plane[:-1]], axis=0)
    below = jnp.concatenate([plane[1:], below_row], axis=0)
    left = jnp.concatenate([zero_col, plane[:, :-1]], axis=1)
    right = jnp.concatenate([plane[:, 1:], zero_col], axis=1)
    beside_all = below + above + right + left
    return plane + KAPPA * (beside_all - 4.0 * plane)


def local(fields, weight_bank, dest_slab, dest_tile, tile_blocks, band_terms):
    peer_count = lax.axis_size("perp")
    plane_count = lax.axis_size("par")
    field_count, _, row_count, col_count = fields.shape
    local_pair = fields[:, 0]
    tile_count = (row_count // TILE) * (col_count // TILE)
    capacity = max(2, (tile_count + peer_count - 1) // peer_count)
    dest_slabs = dest_slab[:, 0, :, 0]
    target = dest_tile[:, 0, :]
    left_index = tile_blocks[:, 0, :, 0]
    right_index = tile_blocks[:, 0, :, 1]

    chosen = slot_labels(dest_slabs, peer_count, capacity)
    tile_ids = (
        jnp.arange(field_count, dtype=jnp.int32)[:, None] * tile_count
        + jnp.arange(tile_count, dtype=jnp.int32)[None, :]
    )
    source_id = jnp.sum(chosen.astype(jnp.int32) * (tile_ids[:, None, None, :] + 1), axis=3) - 1
    source_id = jnp.where(source_id < 0, field_count * tile_count, source_id)
    blocks = jnp.clip(
        jnp.stack((left_index.reshape(-1), right_index.reshape(-1))), 0, weight_bank.shape[0] - 1
    )
    slot_sources = source_id.transpose(1, 2, 0)
    packed = move_and_pack(
        slot_sources.reshape(-1), blocks, local_pair, weight_bank, slot_sources.size
    ).reshape(slot_sources.shape + (TILE, TILE))
    moved_tiles = lax.all_to_all(packed, "perp", split_axis=0, concat_axis=0, tiled=True)
    slot_target = jnp.sum(chosen.astype(jnp.int32) * (target[:, None, None, :] + 1), axis=3) - 1
    arrived_target = lax.all_to_all(
        slot_target.transpose(1, 2, 0), "perp", split_axis=0, concat_axis=0, tiled=True
    )

    labels = jnp.clip(arrived_target.reshape(-1) + 1, 0, tile_count)
    deposit = land(
        labels, moved_tiles.reshape(-1, TILE, TILE), field_count, tile_count, row_count, col_count
    )

    upward = [(i, i + 1) for i in range(plane_count - 1)]
    downward = [(i + 1, i) for i in range(plane_count - 1)]
    mapped = (
        lax.ppermute(deposit[0], "par", upward),
        lax.ppermute(deposit[1], "par", downward),
    )

    forward = [(i, i + 1) for i in range(peer_count - 1)]
    backward = [(i + 1, i) for i in range(peer_count - 1)]
    from_above = lax.ppermute(jnp.stack([m[-1:] for m in mapped]), "perp", forward)
    from_below = lax.ppermute(jnp.stack([m[:1] for m in mapped]), "perp", backward)
    chunk_rows = row_count // plane_count
    sides = []
    for f in range(field_count):
        smoothed = smooth_slab(mapped[f], from_above[f], from_below[f])
        side = local_pair[f] - smoothed
        if f == 1:
            side = -side
        sides.append(side.reshape(plane_count, chunk_rows, col_count))
    right_side = jnp.stack(sides, axis=1)
    column_block = lax.all_to_all(right_side, "par", split_axis=0, concat_axis=0, tiled=True)
    solved = thomas(column_block, band_terms)
    back = lax.all_to_all(solved, "par", split_axis=0, concat_axis=0, tiled=True)
    result = back.transpose(1, 0, 2, 3).reshape(field_count, 1, row_count, col_count)
    return result


def solution(mesh):
    placed = (
        P(None, "par", "perp", None),
        P(),
        P(None, "par", "perp", None),
        P(None, "par", "perp"),
        P(None, "par", "perp", None),
        P(),
    )
    return jax.shard_map(
        local, mesh=mesh, in_specs=placed, out_specs=P(None, "par", "perp", None), check_vma=False
    )
```

```python
import jax
import jax.numpy as jnp
from jax import lax
from jax.experimental import pallas as pl
from jax.experimental.pallas import tpu as pltpu
from jax.sharding import PartitionSpec as P

TILE = 128


PRECISE = lax.Precision.HIGHEST
THREE_PASS = lax.Precision.HIGH
KAPPA = 0.125


def split_tiles(plane_pair):
    field_count, row_count, col_count = plane_pair.shape
    shaped = plane_pair.reshape(field_count, row_count // TILE, TILE, col_count // TILE, TILE)
    return shaped.transpose(0, 1, 3, 2, 4).reshape(field_count, -1, TILE, TILE)


def join_tiles(tile_set, row_count, col_count):
    field_count = tile_set.shape[0]
    shaped = tile_set.reshape(field_count, row_count // TILE, col_count // TILE, TILE, TILE)
    return shaped.transpose(0, 1, 3, 2, 4).reshape(field_count, row_count, col_count)


def slot_labels(dest_slabs, peer_count, capacity):
    tile_count = dest_slabs.shape[-1]
    position = jnp.arange(tile_count, dtype=jnp.int32)
    earlier = position[:, None] > position[None, :]
    shared = dest_slabs[..., :, None] == dest_slabs[..., None, :]
    slot_rank = jnp.sum((shared & earlier).astype(jnp.int32), axis=-1)
    peer_ids = jnp.arange(peer_count, dtype=jnp.int32)
    slot_ids = jnp.arange(capacity, dtype=jnp.int32)
    chosen = (dest_slabs[..., None, None, :] == peer_ids[:, None, None]) & (
        slot_rank[..., None, None, :] == slot_ids[None, :, None]
    )
    return chosen


def thomas_kernel(band_ref, rhs_ref, out_ref, ratio_ref):
    depth = rhs_ref.shape[0]
    shape = rhs_ref.shape[1:]
    ratio = jnp.zeros(shape, jnp.float32)
    previous = jnp.zeros(shape, jnp.float32)
    for p in range(depth):
        lower_now = band_ref[0, p] if p > 0 else 0.0
        upper_now = band_ref[1, p] if p < depth - 1 else 0.0
        pivot = 1.0 - lower_now * ratio
        ratio = upper_now / pivot
        ratio_ref[p] = ratio
        previous = (rhs_ref[p] - lower_now * previous) / pivot
        out_ref[p] = previous
    following = previous
    for p in reversed(range(depth - 1)):
        following = out_ref[p] - ratio_ref[p] * following
        out_ref[p] = following


def thomas(rhs, band_terms):
    scalar = pl.BlockSpec(memory_space=pltpu.SMEM)
    whole = pl.BlockSpec(memory_space=pltpu.VMEM)
    return pl.pallas_call(
        thomas_kernel,
        out_shape=jax.ShapeDtypeStruct(rhs.shape, rhs.dtype),
        in_specs=[scalar, whole],
        out_specs=whole,
        scratch_shapes=[pltpu.VMEM(rhs.shape, jnp.float32)],
    )(band_terms, rhs)


def moving_kernel(source_ref, block_ref, plane_ref, bank_ref, out_ref, moved_ref):
    field_count = plane_ref.shape[0]
    tiles_across = plane_ref.shape[2] // TILE
    tile_count = (plane_ref.shape[1] // TILE) * tiles_across
    blank = field_count * tile_count
    moved_ref[blank] = jnp.zeros((TILE, TILE), jnp.float32)
    for field in range(field_count):
        for s in range(tile_count):
            a, b = divmod(s, tiles_across)
            tile = plane_ref[field, a * TILE:(a + 1) * TILE, b * TILE:(b + 1) * TILE]
            left = bank_ref[block_ref[0, field * tile_count + s]]
            right = bank_ref[block_ref[1, field * tile_count + s]]
            shifted = jnp.dot(left, tile, precision=THREE_PASS, preferred_element_type=jnp.float32)
            moved_ref[field * tile_count + s] = lax.dot_general(
                shifted, right, (((1,), (1,)), ((), ())),
                precision=THREE_PASS, preferred_element_type=jnp.float32,
            )
    for k in range(out_ref.shape[0]):
        out_ref[k] = moved_ref[source_ref[k]]


def move_and_pack(source_ids, blocks, planes, weight_bank, slot_count):
    scalar = pl.BlockSpec(memory_space=pltpu.SMEM)
    whole = pl.BlockSpec(memory_space=pltpu.VMEM)
    field_count, row_count, col_count = planes.shape
    tile_total = field_count * (row_count // TILE) * (col_count // TILE)
    return pl.pallas_call(
        moving_kernel,
        out_shape=jax.ShapeDtypeStruct((slot_count, TILE, TILE), planes.dtype),
        in_specs=[scalar, scalar, whole, whole],
        out_specs=whole,
        scratch_shapes=[pltpu.VMEM((tile_total + 1, TILE, TILE), jnp.float32)],
    )(source_ids, blocks, planes, weight_bank)


def landing_kernel(label_ref, recv_ref, out_ref, acc_ref):
    field_count = out_ref.shape[0]
    tiles_across = out_ref.shape[2] // TILE
    acc_ref[...] = jnp.zeros(acc_ref.shape, jnp.float32)
    for k in range(recv_ref.shape[0]):
        field = k % field_count
        label = label_ref[k]
        acc_ref[field, label] = acc_ref[field, label] + recv_ref[k]
    for field in range(field_count):
        for t in range(acc_ref.shape[1] - 1):
            a, b = divmod(t, tiles_across)
            out_ref[field, a * TILE:(a + 1) * TILE, b * TILE:(b + 1) * TILE] = acc_ref[field, t + 1]


def land(labels, received, field_count, tile_count, row_count, col_count):
    scalar = pl.BlockSpec(memory_space=pltpu.SMEM)
    whole = pl.BlockSpec(memory_space=pltpu.VMEM)
    return pl.pallas_call(
        landing_kernel,
        out_shape=jax.ShapeDtypeStruct((field_count, row_count, col_count), received.dtype),
        in_specs=[scalar, whole],
        out_specs=whole,
        scratch_shapes=[pltpu.VMEM((field_count, tile_count + 1, TILE, TILE), jnp.float32)],
    )(labels, received)


def smooth_slab(plane, above_row, below_row):
    row_count, col_count = plane.shape
    zero_col = jnp.zeros((row_count, 1), plane.dtype)
    above = jnp.concatenate([above_row, plane[:-1]], axis=0)
    below = jnp.concatenate([plane[1:], below_row], axis=0)
    left = jnp.concatenate([zero_col, plane[:, :-1]], axis=1)
    right = jnp.concatenate([plane[:, 1:], zero_col], axis=1)
    beside_all = below + above + right + left
    return plane + KAPPA * (beside_all - 4.0 * plane)


def local(fields, weight_bank, dest_slab, dest_tile, tile_blocks, band_terms):
    peer_count = lax.axis_size("perp")
    plane_count = lax.axis_size("par")
    field_count, _, row_count, col_count = fields.shape
    local_pair = fields[:, 0]
    tile_count = (row_count // TILE) * (col_count // TILE)
    capacity = max(2, (tile_count + peer_count - 1) // peer_count)
    dest_slabs = dest_slab[:, 0, :, 0]
    target = dest_tile[:, 0, :]
    left_index = tile_blocks[:, 0, :, 0]
    right_index = tile_blocks[:, 0, :, 1]

    chosen = slot_labels(dest_slabs, peer_count, capacity)
    tile_ids = (
        jnp.arange(field_count, dtype=jnp.int32)[:, None] * tile_count
        + jnp.arange(tile_count, dtype=jnp.int32)[None, :]
    )
    source_id = jnp.sum(chosen.astype(jnp.int32) * (tile_ids[:, None, None, :] + 1), axis=3) - 1
    source_id = jnp.where(source_id < 0, field_count * tile_count, source_id)
    blocks = jnp.clip(
        jnp.stack((left_index.reshape(-1), right_index.reshape(-1))), 0, weight_bank.shape[0] - 1
    )
    slot_sources = source_id.transpose(1, 2, 0)
    packed = move_and_pack(
        slot_sources.reshape(-1), blocks, local_pair, weight_bank, slot_sources.size
    ).reshape(slot_sources.shape + (TILE, TILE))
    moved_tiles = lax.all_to_all(packed, "perp", split_axis=0, concat_axis=0, tiled=True)
    slot_target = jnp.sum(chosen.astype(jnp.int32) * (target[:, None, None, :] + 1), axis=3) - 1
    arrived_target = lax.all_to_all(
        slot_target.transpose(1, 2, 0), "perp", split_axis=0, concat_axis=0, tiled=True
    )

    labels = jnp.clip(arrived_target.reshape(-1) + 1, 0, tile_count)
    deposit = land(
        labels, moved_tiles.reshape(-1, TILE, TILE), field_count, tile_count, row_count, col_count
    )

    upward = [(i, i + 1) for i in range(plane_count - 1)]
    downward = [(i + 1, i) for i in range(plane_count - 1)]
    mapped = (
        lax.ppermute(deposit[0], "par", upward),
        lax.ppermute(deposit[1], "par", downward),
    )

    forward = [(i, i + 1) for i in range(peer_count - 1)]
    backward = [(i + 1, i) for i in range(peer_count - 1)]
    from_above = lax.ppermute(jnp.stack([m[-1:] for m in mapped]), "perp", forward)
    from_below = lax.ppermute(jnp.stack([m[:1] for m in mapped]), "perp", backward)
    chunk_rows = row_count // plane_count
    sides = []
    for f in range(field_count):
        smoothed = smooth_slab(mapped[f], from_above[f], from_below[f])
        side = local_pair[f] - smoothed
        if f == 1:
            side = -side
        sides.append(side.reshape(plane_count, chunk_rows, col_count))
    right_side = jnp.stack(sides, axis=1)
    column_block = lax.all_to_all(right_side, "par", split_axis=0, concat_axis=0, tiled=True)
    solved = thomas(column_block, band_terms)
    back = lax.all_to_all(solved, "par", split_axis=0, concat_axis=0, tiled=True)
    result = back.transpose(1, 0, 2, 3).reshape(field_count, 1, row_count, col_count)
    return result


def solution(mesh):
    placed = (
        P(None, "par", "perp", None),
        P(),
        P(None, "par", "perp", None),
        P(None, "par", "perp"),
        P(None, "par", "perp", None),
        P(),
    )
    return jax.shard_map(
        local, mesh=mesh, in_specs=placed, out_specs=P(None, "par", "perp", None), check_vma=False
    )
```

```python
import jax
import jax.numpy as jnp
from jax import lax
from jax.experimental import pallas as pl
from jax.experimental.pallas import tpu as pltpu
from jax.sharding import PartitionSpec as P

TILE = 128


PRECISE = lax.Precision.HIGHEST
THREE_PASS = lax.Precision.HIGH
KAPPA = 0.125


def split_tiles(plane_pair):
    field_count, row_count, col_count = plane_pair.shape
    shaped = plane_pair.reshape(field_count, row_count // TILE, TILE, col_count // TILE, TILE)
    return shaped.transpose(0, 1, 3, 2, 4).reshape(field_count, -1, TILE, TILE)


def join_tiles(tile_set, row_count, col_count):
    field_count = tile_set.shape[0]
    shaped = tile_set.reshape(field_count, row_count // TILE, col_count // TILE, TILE, TILE)
    return shaped.transpose(0, 1, 3, 2, 4).reshape(field_count, row_count, col_count)


def slot_labels(dest_slabs, peer_count, capacity):
    tile_count = dest_slabs.shape[-1]
    position = jnp.arange(tile_count, dtype=jnp.int32)
    earlier = position[:, None] > position[None, :]
    shared = dest_slabs[..., :, None] == dest_slabs[..., None, :]
    slot_rank = jnp.sum((shared & earlier).astype(jnp.int32), axis=-1)
    peer_ids = jnp.arange(peer_count, dtype=jnp.int32)
    slot_ids = jnp.arange(capacity, dtype=jnp.int32)
    chosen = (dest_slabs[..., None, None, :] == peer_ids[:, None, None]) & (
        slot_rank[..., None, None, :] == slot_ids[None, :, None]
    )
    return chosen


def thomas_kernel(band_ref, rhs_ref, out_ref, ratio_ref):
    depth = rhs_ref.shape[0]
    shape = rhs_ref.shape[1:]
    ratio = jnp.zeros(shape, jnp.float32)
    previous = jnp.zeros(shape, jnp.float32)
    for p in range(depth):
        lower_now = band_ref[0, p] if p > 0 else 0.0
        upper_now = band_ref[1, p] if p < depth - 1 else 0.0
        pivot = 1.0 - lower_now * ratio
        ratio = upper_now / pivot
        ratio_ref[p] = ratio
        previous = (rhs_ref[p] - lower_now * previous) / pivot
        out_ref[p] = previous
    following = previous
    for p in reversed(range(depth - 1)):
        following = out_ref[p] - ratio_ref[p] * following
        out_ref[p] = following


def thomas(rhs, band_terms):
    scalar = pl.BlockSpec(memory_space=pltpu.SMEM)
    whole = pl.BlockSpec(memory_space=pltpu.VMEM)
    return pl.pallas_call(
        thomas_kernel,
        out_shape=jax.ShapeDtypeStruct(rhs.shape, rhs.dtype),
        in_specs=[scalar, whole],
        out_specs=whole,
        scratch_shapes=[pltpu.VMEM(rhs.shape, jnp.float32)],
    )(band_terms, rhs)


def moving_kernel(source_ref, block_ref, plane_ref, bank_ref, out_ref, moved_ref):
    field_count = plane_ref.shape[0]
    tiles_across = plane_ref.shape[2] // TILE
    tile_count = (plane_ref.shape[1] // TILE) * tiles_across
    blank = field_count * tile_count
    moved_ref[blank] = jnp.zeros((TILE, TILE), jnp.float32)
    for field in range(field_count):
        for s in range(tile_count):
            a, b = divmod(s, tiles_across)
            tile = plane_ref[field, a * TILE:(a + 1) * TILE, b * TILE:(b + 1) * TILE]
            left = bank_ref[block_ref[0, field * tile_count + s]]
            right = bank_ref[block_ref[1, field * tile_count + s]]
            shifted = jnp.dot(left, tile, precision=THREE_PASS, preferred_element_type=jnp.float32)
            moved_ref[field * tile_count + s] = lax.dot_general(
                shifted, right, (((1,), (1,)), ((), ())),
                precision=THREE_PASS, preferred_element_type=jnp.float32,
            )
    for k in range(out_ref.shape[0]):
        out_ref[k] = moved_ref[source_ref[k]]


def move_and_pack(source_ids, blocks, planes, weight_bank, slot_count):
    scalar = pl.BlockSpec(memory_space=pltpu.SMEM)
    whole = pl.BlockSpec(memory_space=pltpu.VMEM)
    field_count, row_count, col_count = planes.shape
    tile_total = field_count * (row_count // TILE) * (col_count // TILE)
    return pl.pallas_call(
        moving_kernel,
        out_shape=jax.ShapeDtypeStruct((slot_count, TILE, TILE), planes.dtype),
        in_specs=[scalar, scalar, whole, whole],
        out_specs=whole,
        scratch_shapes=[pltpu.VMEM((tile_total + 1, TILE, TILE), jnp.float32)],
    )(source_ids, blocks, planes, weight_bank)


def landing_kernel(label_ref, recv_ref, *refs):
    out_refs, acc_ref = refs[:-1], refs[-1]
    field_count = len(out_refs)
    tiles_across = out_refs[0].shape[1] // TILE
    acc_ref[...] = jnp.zeros(acc_ref.shape, jnp.float32)
    for k in range(recv_ref.shape[0]):
        field = k % field_count
        label = label_ref[k]
        acc_ref[field, label] = acc_ref[field, label] + recv_ref[k]
    for field in range(field_count):
        for t in range(acc_ref.shape[1] - 1):
            a, b = divmod(t, tiles_across)
            out_refs[field][a * TILE:(a + 1) * TILE, b * TILE:(b + 1) * TILE] = acc_ref[field, t + 1]


def land(labels, received, field_count, tile_count, row_count, col_count):
    scalar = pl.BlockSpec(memory_space=pltpu.SMEM)
    whole = pl.BlockSpec(memory_space=pltpu.VMEM)
    return pl.pallas_call(
        landing_kernel,
        out_shape=tuple(
            jax.ShapeDtypeStruct((row_count, col_count), received.dtype) for _ in range(field_count)
        ),
        in_specs=[scalar, whole],
        out_specs=tuple(whole for _ in range(field_count)),
        scratch_shapes=[pltpu.VMEM((field_count, tile_count + 1, TILE, TILE), jnp.float32)],
    )(labels, received)


def smooth_slab(plane, above_row, below_row):
    row_count, col_count = plane.shape
    zero_col = jnp.zeros((row_count, 1), plane.dtype)
    above = jnp.concatenate([above_row, plane[:-1]], axis=0)
    below = jnp.concatenate([plane[1:], below_row], axis=0)
    left = jnp.concatenate([zero_col, plane[:, :-1]], axis=1)
    right = jnp.concatenate([plane[:, 1:], zero_col], axis=1)
    beside_all = below + above + right + left
    return plane + KAPPA * (beside_all - 4.0 * plane)


def local(fields, weight_bank, dest_slab, dest_tile, tile_blocks, band_terms):
    peer_count = lax.axis_size("perp")
    plane_count = lax.axis_size("par")
    field_count, _, row_count, col_count = fields.shape
    local_pair = fields[:, 0]
    tile_count = (row_count // TILE) * (col_count // TILE)
    capacity = max(2, (tile_count + peer_count - 1) // peer_count)
    dest_slabs = dest_slab[:, 0, :, 0]
    target = dest_tile[:, 0, :]
    left_index = tile_blocks[:, 0, :, 0]
    right_index = tile_blocks[:, 0, :, 1]

    chosen = slot_labels(dest_slabs, peer_count, capacity)
    tile_ids = (
        jnp.arange(field_count, dtype=jnp.int32)[:, None] * tile_count
        + jnp.arange(tile_count, dtype=jnp.int32)[None, :]
    )
    source_id = jnp.sum(chosen.astype(jnp.int32) * (tile_ids[:, None, None, :] + 1), axis=3) - 1
    source_id = jnp.where(source_id < 0, field_count * tile_count, source_id)
    blocks = jnp.clip(
        jnp.stack((left_index.reshape(-1), right_index.reshape(-1))), 0, weight_bank.shape[0] - 1
    )
    slot_sources = source_id.transpose(1, 2, 0)
    packed = move_and_pack(
        slot_sources.reshape(-1), blocks, local_pair, weight_bank, slot_sources.size
    ).reshape(slot_sources.shape + (TILE, TILE))
    moved_tiles = lax.all_to_all(packed, "perp", split_axis=0, concat_axis=0, tiled=True)
    slot_target = jnp.sum(chosen.astype(jnp.int32) * (target[:, None, None, :] + 1), axis=3) - 1
    arrived_target = lax.all_to_all(
        slot_target.transpose(1, 2, 0), "perp", split_axis=0, concat_axis=0, tiled=True
    )

    labels = jnp.clip(arrived_target.reshape(-1) + 1, 0, tile_count)
    deposit = land(
        labels, moved_tiles.reshape(-1, TILE, TILE), field_count, tile_count, row_count, col_count
    )

    upward = [(i, i + 1) for i in range(plane_count - 1)]
    downward = [(i + 1, i) for i in range(plane_count - 1)]
    mapped = (
        lax.ppermute(deposit[0], "par", upward),
        lax.ppermute(deposit[1], "par", downward),
    )

    forward = [(i, i + 1) for i in range(peer_count - 1)]
    backward = [(i + 1, i) for i in range(peer_count - 1)]
    from_above = lax.ppermute(jnp.stack([m[-1:] for m in mapped]), "perp", forward)
    from_below = lax.ppermute(jnp.stack([m[:1] for m in mapped]), "perp", backward)
    chunk_rows = row_count // plane_count
    sides = []
    for f in range(field_count):
        smoothed = smooth_slab(mapped[f], from_above[f], from_below[f])
        side = local_pair[f] - smoothed
        if f == 1:
            side = -side
        sides.append(side.reshape(plane_count, chunk_rows, col_count))
    right_side = jnp.stack(sides, axis=1)
    column_block = lax.all_to_all(right_side, "par", split_axis=0, concat_axis=0, tiled=True)
    solved = thomas(column_block, band_terms)
    back = lax.all_to_all(solved, "par", split_axis=0, concat_axis=0, tiled=True)
    result = back.transpose(1, 0, 2, 3).reshape(field_count, 1, row_count, col_count)
    return result


def solution(mesh):
    placed = (
        P(None, "par", "perp", None),
        P(),
        P(None, "par", "perp", None),
        P(None, "par", "perp"),
        P(None, "par", "perp", None),
        P(),
    )
    return jax.shard_map(
        local, mesh=mesh, in_specs=placed, out_specs=P(None, "par", "perp", None), check_vma=False
    )
```

```python
import jax
import jax.numpy as jnp
from jax import lax
from jax.experimental import pallas as pl
from jax.experimental.pallas import tpu as pltpu
from jax.sharding import PartitionSpec as P

TILE = 128


PRECISE = lax.Precision.HIGHEST
THREE_PASS = lax.Precision.HIGH
KAPPA = 0.125


def split_tiles(plane_pair):
    field_count, row_count, col_count = plane_pair.shape
    shaped = plane_pair.reshape(field_count, row_count // TILE, TILE, col_count // TILE, TILE)
    return shaped.transpose(0, 1, 3, 2, 4).reshape(field_count, -1, TILE, TILE)


def join_tiles(tile_set, row_count, col_count):
    field_count = tile_set.shape[0]
    shaped = tile_set.reshape(field_count, row_count // TILE, col_count // TILE, TILE, TILE)
    return shaped.transpose(0, 1, 3, 2, 4).reshape(field_count, row_count, col_count)


def slot_labels(dest_slabs, peer_count, capacity):
    tile_count = dest_slabs.shape[-1]
    position = jnp.arange(tile_count, dtype=jnp.int32)
    earlier = position[:, None] > position[None, :]
    shared = dest_slabs[..., :, None] == dest_slabs[..., None, :]
    slot_rank = jnp.sum((shared & earlier).astype(jnp.int32), axis=-1)
    peer_ids = jnp.arange(peer_count, dtype=jnp.int32)
    slot_ids = jnp.arange(capacity, dtype=jnp.int32)
    chosen = (dest_slabs[..., None, None, :] == peer_ids[:, None, None]) & (
        slot_rank[..., None, None, :] == slot_ids[None, :, None]
    )
    return chosen


def thomas_kernel(band_ref, rhs_ref, out_ref, ratio_ref):
    depth = rhs_ref.shape[0]
    shape = rhs_ref.shape[1:]
    ratio = jnp.zeros(shape, jnp.float32)
    previous = jnp.zeros(shape, jnp.float32)
    for p in range(depth):
        lower_now = band_ref[0, p] if p > 0 else 0.0
        upper_now = band_ref[1, p] if p < depth - 1 else 0.0
        pivot = 1.0 - lower_now * ratio
        ratio = upper_now / pivot
        ratio_ref[p] = ratio
        previous = (rhs_ref[p] - lower_now * previous) / pivot
        out_ref[p] = previous
    following = previous
    for p in reversed(range(depth - 1)):
        following = out_ref[p] - ratio_ref[p] * following
        out_ref[p] = following


def thomas(rhs, band_terms):
    scalar = pl.BlockSpec(memory_space=pltpu.SMEM)
    whole = pl.BlockSpec(memory_space=pltpu.VMEM)
    return pl.pallas_call(
        thomas_kernel,
        out_shape=jax.ShapeDtypeStruct(rhs.shape, rhs.dtype),
        in_specs=[scalar, whole],
        out_specs=whole,
        scratch_shapes=[pltpu.VMEM(rhs.shape, jnp.float32)],
    )(band_terms, rhs)


def moving_kernel(slot_ref, block_ref, plane_ref, bank_ref, out_ref):
    field_count = plane_ref.shape[0]
    tiles_across = plane_ref.shape[2] // TILE
    tile_count = (plane_ref.shape[1] // TILE) * tiles_across
    out_ref[...] = jnp.zeros(out_ref.shape, jnp.float32)
    for field in range(field_count):
        for s in range(tile_count):
            a, b = divmod(s, tiles_across)
            tile = plane_ref[field, a * TILE:(a + 1) * TILE, b * TILE:(b + 1) * TILE]
            left = bank_ref[block_ref[0, field * tile_count + s]]
            right = bank_ref[block_ref[1, field * tile_count + s]]
            shifted = jnp.dot(left, tile, precision=THREE_PASS, preferred_element_type=jnp.float32)
            out_ref[slot_ref[field * tile_count + s]] = lax.dot_general(
                shifted, right, (((1,), (1,)), ((), ())),
                precision=THREE_PASS, preferred_element_type=jnp.float32,
            )


def move_and_pack(slot_ids, blocks, planes, weight_bank, slot_count):
    scalar = pl.BlockSpec(memory_space=pltpu.SMEM)
    whole = pl.BlockSpec(memory_space=pltpu.VMEM)
    return pl.pallas_call(
        moving_kernel,
        out_shape=jax.ShapeDtypeStruct((slot_count, TILE, TILE), planes.dtype),
        in_specs=[scalar, scalar, whole, whole],
        out_specs=whole,
    )(slot_ids, blocks, planes, weight_bank)


def landing_kernel(label_ref, recv_ref, *refs):
    out_refs, acc_ref = refs[:-1], refs[-1]
    field_count = len(out_refs)
    tiles_across = out_refs[0].shape[1] // TILE
    acc_ref[...] = jnp.zeros(acc_ref.shape, jnp.float32)
    for k in range(recv_ref.shape[0]):
        field = k % field_count
        label = label_ref[k]
        acc_ref[field, label] = acc_ref[field, label] + recv_ref[k]
    for field in range(field_count):
        for t in range(acc_ref.shape[1] - 1):
            a, b = divmod(t, tiles_across)
            out_refs[field][a * TILE:(a + 1) * TILE, b * TILE:(b + 1) * TILE] = acc_ref[field, t + 1]


def land(labels, received, field_count, tile_count, row_count, col_count):
    scalar = pl.BlockSpec(memory_space=pltpu.SMEM)
    whole = pl.BlockSpec(memory_space=pltpu.VMEM)
    return pl.pallas_call(
        landing_kernel,
        out_shape=tuple(
            jax.ShapeDtypeStruct((row_count, col_count), received.dtype) for _ in range(field_count)
        ),
        in_specs=[scalar, whole],
        out_specs=tuple(whole for _ in range(field_count)),
        scratch_shapes=[pltpu.VMEM((field_count, tile_count + 1, TILE, TILE), jnp.float32)],
    )(labels, received)


def smooth_slab(plane, above_row, below_row):
    row_count, col_count = plane.shape
    zero_col = jnp.zeros((row_count, 1), plane.dtype)
    above = jnp.concatenate([above_row, plane[:-1]], axis=0)
    below = jnp.concatenate([plane[1:], below_row], axis=0)
    left = jnp.concatenate([zero_col, plane[:, :-1]], axis=1)
    right = jnp.concatenate([plane[:, 1:], zero_col], axis=1)
    beside_all = below + above + right + left
    return plane + KAPPA * (beside_all - 4.0 * plane)


def local(fields, weight_bank, dest_slab, dest_tile, tile_blocks, band_terms):
    peer_count = lax.axis_size("perp")
    plane_count = lax.axis_size("par")
    field_count, _, row_count, col_count = fields.shape
    local_pair = fields[:, 0]
    tile_count = (row_count // TILE) * (col_count // TILE)
    capacity = max(2, (tile_count + peer_count - 1) // peer_count)
    dest_slabs = dest_slab[:, 0, :, 0]
    target = dest_tile[:, 0, :]
    left_index = tile_blocks[:, 0, :, 0]
    right_index = tile_blocks[:, 0, :, 1]

    chosen = slot_labels(dest_slabs, peer_count, capacity)
    slot_ids = jnp.arange(peer_count * capacity, dtype=jnp.int32).reshape(peer_count, capacity)
    slot_ids = slot_ids[None] * field_count + jnp.arange(field_count, dtype=jnp.int32)[:, None, None]
    tile_slot = jnp.sum(chosen.astype(jnp.int32) * slot_ids[..., None], axis=(1, 2))
    slot_count = peer_count * capacity * field_count
    tile_slot = jnp.clip(tile_slot, 0, slot_count - 1)
    blocks = jnp.clip(
        jnp.stack((left_index.reshape(-1), right_index.reshape(-1))), 0, weight_bank.shape[0] - 1
    )
    packed = move_and_pack(
        tile_slot.reshape(-1), blocks, local_pair, weight_bank, slot_count
    ).reshape(peer_count, capacity, field_count, TILE, TILE)
    moved_tiles = lax.all_to_all(packed, "perp", split_axis=0, concat_axis=0, tiled=True)
    slot_target = jnp.sum(chosen.astype(jnp.int32) * (target[:, None, None, :] + 1), axis=3) - 1
    arrived_target = lax.all_to_all(
        slot_target.transpose(1, 2, 0), "perp", split_axis=0, concat_axis=0, tiled=True
    )

    labels = jnp.clip(arrived_target.reshape(-1) + 1, 0, tile_count)
    deposit = land(
        labels, moved_tiles.reshape(-1, TILE, TILE), field_count, tile_count, row_count, col_count
    )

    upward = [(i, i + 1) for i in range(plane_count - 1)]
    downward = [(i + 1, i) for i in range(plane_count - 1)]
    mapped = (
        lax.ppermute(deposit[0], "par", upward),
        lax.ppermute(deposit[1], "par", downward),
    )

    forward = [(i, i + 1) for i in range(peer_count - 1)]
    backward = [(i + 1, i) for i in range(peer_count - 1)]
    from_above = lax.ppermute(jnp.stack([m[-1:] for m in mapped]), "perp", forward)
    from_below = lax.ppermute(jnp.stack([m[:1] for m in mapped]), "perp", backward)
    chunk_rows = row_count // plane_count
    sides = []
    for f in range(field_count):
        smoothed = smooth_slab(mapped[f], from_above[f], from_below[f])
        side = local_pair[f] - smoothed
        if f == 1:
            side = -side
        sides.append(side.reshape(plane_count, chunk_rows, col_count))
    right_side = jnp.stack(sides, axis=1)
    column_block = lax.all_to_all(right_side, "par", split_axis=0, concat_axis=0, tiled=True)
    solved = thomas(column_block, band_terms)
    back = lax.all_to_all(solved, "par", split_axis=0, concat_axis=0, tiled=True)
    result = back.transpose(1, 0, 2, 3).reshape(field_count, 1, row_count, col_count)
    return result


def solution(mesh):
    placed = (
        P(None, "par", "perp", None),
        P(),
        P(None, "par", "perp", None),
        P(None, "par", "perp"),
        P(None, "par", "perp", None),
        P(),
    )
    return jax.shard_map(
        local, mesh=mesh, in_specs=placed, out_specs=P(None, "par", "perp", None), check_vma=False
    )
```
